256 devices in a mesh: lon: 16 (over z, core), lat: 16 (over x, y).
Axes of the slice: x: 4, y: 4, z: 8, core: 2. Of those that a mesh axis runs over, the one named last changes fastest.
Arguments:
- state: float32 [16, 512, 4096], P(None, 'lat', 'lon'), may hold values from -6 to 6
- coef_lon: float32 [512, 4096], P('lat', 'lon'), may hold values from 0.2 to 0.24
- coef_lat: float32 [512, 4096], P('lat', 'lon'), may hold values from 0.2 to 0.24
- land_sea: int32 [512, 4096], P('lat', 'lon'), may hold values 0 or 1
- send_cols: int32 [16, 65536], P('lat', 'lon'), may hold values from 0 to 8191
- send_count: int32 [16, 256], P('lat', 'lon'), may hold values from 32 to 256, as said below
- obs_value: float32 [16, 16, 65536], P(None, 'lat', 'lon'), may hold values from -6 to 6
- obs_weight: float32 [16, 16, 65536], P(None, 'lat', 'lon'), may hold values from 0.25 to 4
Outputs:
- increment: float32 [16, 512, 4096], P(None, 'lat', 'lon')
The draws below stay inside these ranges and needn't reach their ends.
Inputs may be any that keep to these rules, and one draw needn't show every extreme that they name: `send_count`: at most 256 live slots go from one device to one peer; in every latitude band some receiving device gets 256 from every device of the band, which one drawn from the seed. `send_cols`: entries index a column of the sending device's own block, row-major over its 32 x 256 cells.
All inputs are finite; a program needn't handle non-finite values. No bound on the sum of `land_sea` on one device may be relied on, other than what follows from the above.
Results may differ from the reference program's by a relative error of at most 0.00002.
Values sent between devices are 32-bit elements; how exact they have to be, the bound alone decides.
No kernel may reach another device: no remote copies, remote signals or barrier semaphores. Data moves between devices by JAX's collectives and lax.ppermute only.
A program may use at most 64 MiB of HBM per device.

```python
import math
import jax
import jax.numpy as jnp
from jax import lax

LEV = 16
CLAT = 32
CLON = 256
SLOTS_DEV = 4096
PASSES = 8
CAP = 256
NLAT = 512
NLON = 4096
N_LON = 16
N_LAT = 16


def draw_send_count(key, part):
    capacity = SLOTS_DEV // N_LON
    base_load = jax.random.randint(jax.random.fold_in(key, 11), (N_LAT, N_LON, N_LON), capacity // 8, 3 * capacity // 4 + 1)
    busiest = jax.random.randint(jax.random.fold_in(key, 12), (N_LAT, 1, 1), 0, N_LON)
    dest_index = jnp.arange(N_LON, dtype=jnp.int32)[None, None, :]
    loads = jnp.where(dest_index == busiest, capacity, base_load)
    return loads.reshape(N_LAT, N_LON * N_LON).astype(jnp.int32)


def with_ends(drawn, key, smallest, largest):
    longest = drawn.shape.index(max(drawn.shape))
    spots = []
    for shift in (0, 1):
        where = [jax.random.randint(jax.random.fold_in(key, axis), (), 0, length) for axis, length in enumerate(drawn.shape)]
        where[longest] = (where[longest] + shift) % drawn.shape[longest]
        spots.append(tuple(where))
    return drawn.at[spots[0]].set(smallest).at[spots[1]].set(largest)


def steps_of(stream_key, extent, shards, least, top_value):
    def one(dim, shards_of):
        steps = jax.random.uniform(jax.random.fold_in(jax.random.fold_in(stream_key, 6), dim), (shards_of,), jnp.float32, least / len(shards), top_value / len(shards))
        return jnp.repeat(jnp.exp(steps), extent[dim] // shards_of).reshape((-1,) + (1,) * (len(extent) - dim - 1))

    gain = one(*shards[0])
    for cut in shards[1:]:
        gain = gain * one(*cut)
    return gain


def noise(stream_key, shape, scale, bound, pieces=(), held_as=jnp.bfloat16):
    values = jax.random.normal(stream_key, shape, jnp.float32) * scale
    if len(pieces) > 0:
        values = steps_of(stream_key, shape, pieces, -0.22, 0.18) * values
    return jnp.clip(values, min=-bound, max=bound).astype(held_as)


def setup_inputs(seed: int = 0) -> dict:
    seeds = jax.random.split(jax.random.key(seed), 9)
    state = noise(seeds[0], (LEV, NLAT, NLON), 1.0, 6.0, ((1, 16), (2, 16)), jnp.float32)
    coef_lon = jnp.clip(0.2 + 0.03999999 * jax.random.uniform(seeds[1], (NLAT, NLON), jnp.float32) ** steps_of(seeds[1], (NLAT, NLON), ((0, 16), (1, 16)), -0.2, 0.2), 0.2, 0.24)
    coef_lat = jnp.clip(0.2 + 0.03999999 * jax.random.uniform(seeds[2], (NLAT, NLON), jnp.float32) ** steps_of(seeds[2], (NLAT, NLON), ((0, 16), (1, 16)), -0.2, 0.2), 0.2, 0.24)
    land_sea = with_ends((jax.random.randint(seeds[3], (NLAT, NLON), 0, 20) < 19).astype(jnp.int32), jax.random.fold_in(seeds[3], 1), 0, 1)
    send_cols = with_ends(jax.random.randint(seeds[4], (N_LAT, N_LON * SLOTS_DEV), 0, CLAT * CLON), jax.random.fold_in(seeds[4], 1), 0, (CLAT * CLON) - 1).astype(jnp.int32)
    send_count = draw_send_count(jax.random.fold_in(seeds[8], 71), 0)
    obs_value = noise(seeds[6], (LEV, N_LAT, N_LON * SLOTS_DEV), 1.0, 6.0, ((1, 16), (2, 16)), jnp.float32)
    obs_weight = jnp.clip(jnp.exp(math.log(4.0) - 2.7725887 * jax.random.uniform(seeds[7], (LEV, N_LAT, N_LON * SLOTS_DEV), jnp.float32) ** steps_of(seeds[7], (LEV, N_LAT, N_LON * SLOTS_DEV), ((1, 16), (2, 16)), -0.2, 0.2)), 0.25, 4.0)
    return dict(state=state, coef_lon=coef_lon, coef_lat=coef_lat, land_sea=land_sea, send_cols=send_cols, send_count=send_count, obs_value=obs_value, obs_weight=obs_weight)


def reference(state, coef_lon, coef_lat, land_sea, send_cols, send_count, obs_value, obs_weight):
    targets = send_cols.reshape(N_LAT, N_LON, SLOTS_DEV)
    band_index = jnp.arange(N_LAT, dtype=jnp.int32)[:, None, None]
    owner_index = jnp.arange(N_LON, dtype=jnp.int32)[None, :, None]
    glob_rows = band_index * CLAT + targets // CLON
    glob_cols = owner_index * CLON + targets % CLON
    flat_index = (glob_rows * NLON + glob_cols).reshape(-1).astype(jnp.int32)
    columns = state.reshape(LEV, NLAT * NLON)
    seen = jnp.take(columns, flat_index, axis=1).reshape(LEV, N_LAT, N_LON, N_LON, CAP)
    values = jnp.transpose(obs_value.reshape(LEV, N_LAT, N_LON, N_LON, CAP), (0, 1, 3, 2, 4))
    weights = jnp.transpose(obs_weight.reshape(LEV, N_LAT, N_LON, N_LON, CAP), (0, 1, 3, 2, 4))
    slot_index = jnp.arange(CAP, dtype=jnp.int32)
    counts = send_count.reshape(N_LAT, N_LON, N_LON)
    usable = jnp.where(slot_index[None, None, None, :] < counts[..., None], 1.0, 0.0).astype(jnp.float32)
    weighted = weights * (values - seen) * usable[None]
    gradient = jnp.zeros((LEV, NLAT * NLON), jnp.float32).at[:, flat_index].add(weighted.reshape(LEV, -1))
    sea = land_sea.astype(jnp.float32)
    gradient = gradient.reshape(LEV, NLAT, NLON) * sea[None]
    east_face = coef_lon * sea * jnp.roll(sea, -1, axis=1)
    zero_row = jnp.zeros((1, NLON), jnp.float32)
    north_face = coef_lat * sea * jnp.concatenate([sea[1:], zero_row], axis=0)

    def diffuse(layer_field):
        for step_number in range(PASSES):
            flux_east = east_face * (jnp.roll(layer_field, -1, axis=1) - layer_field)
            upper = jnp.concatenate([layer_field[1:], zero_row], axis=0)
            flux_north = north_face * (upper - layer_field)
            flux_west = jnp.roll(flux_east, 1, axis=1)
            flux_south = jnp.concatenate([zero_row, flux_north[:-1]], axis=0)
            layer_field = layer_field + flux_east - flux_west + flux_north - flux_south
        return layer_field

    return lax.map(diffuse, gradient)
```

```python
import jax
import jax.numpy as jnp
from jax import lax
from jax.sharding import PartitionSpec as P

PASSES = 8


def with_halo(block, sides, width):
    for axis, dim in sides:
        count = lax.axis_size(axis)
        forward = [(i, i + 1) for i in range(count - 1)]
        forward.append((count - 1, 0))
        backward = [(target, source) for source, target in forward]
        low = lax.ppermute(
            lax.slice_in_dim(block, block.shape[dim] - width, None, axis=dim), axis, forward
        )
        high = lax.ppermute(lax.slice_in_dim(block, 0, width, axis=dim), axis, backward)
        block = jnp.concatenate([low, block, high], axis=dim)
    return block


def one_pass(layer_field, east_face, north_face):
    flux_east = east_face * (layer_field[:, :, 1:] - layer_field[:, :, :-1])
    flux_north = north_face * (layer_field[:, 1:, :] - layer_field[:, :-1, :])
    return (
        layer_field[:, 1:-1, 1:-1]
        + flux_east[:, 1:-1, 1:]
        - flux_east[:, 1:-1, :-1]
        + flux_north[:, 1:, 1:-1]
        - flux_north[:, :-1, 1:-1]
    )


def body(state, coef_lon, coef_lat, land_sea, send_cols, send_count, obs_value, obs_weight):
    levels, rows_here, cols_here = state.shape
    lon_count = lax.axis_size("lon")
    lat_count = lax.axis_size("lat")
    slots = send_cols.shape[1]
    capacity = slots // lon_count
    columns = state.reshape(levels, rows_here * cols_here)
    targets = send_cols[0]
    slot_index = jnp.arange(slots, dtype=jnp.int32)
    limits = jnp.broadcast_to(send_count[0][:, None], (lon_count, capacity)).reshape(slots)
    usable = jnp.where(slot_index % capacity < limits, 1.0, 0.0).astype(jnp.float32)
    at_column = jnp.take(columns, targets, axis=1)
    remote = lax.all_to_all(at_column, "lon", split_axis=1, concat_axis=1, tiled=True)
    local_terms = obs_weight[:, 0, :] * (obs_value[:, 0, :] - remote)
    weighted = lax.all_to_all(local_terms, "lon", split_axis=1, concat_axis=1, tiled=True) * usable
    sea = land_sea.astype(jnp.float32)
    gradient = jnp.zeros((levels, rows_here * cols_here), jnp.float32).at[:, targets].add(weighted)
    gradient = gradient.reshape(levels, rows_here, cols_here) * sea[None]
    rim_width = PASSES
    stacked = jnp.stack([sea, coef_lon, coef_lat])
    padded = with_halo(stacked, (("lon", 2), ("lat", 1)), rim_width)
    lat_index = lax.axis_index("lat")
    row_place = jnp.arange(rows_here + 2 * rim_width, dtype=jnp.int32)
    outside = (row_place < rim_width) & (lat_index == 0) | (row_place >= rows_here + rim_width) & (
        lat_index == lat_count - 1
    )
    inside = jnp.where(outside, 0.0, 1.0).astype(jnp.float32)[:, None]
    sea_rim = padded[0] * inside
    east_face = padded[1][:, :-1] * sea_rim[:, :-1] * sea_rim[:, 1:]
    north_face = padded[2][:-1, :] * sea_rim[:-1, :] * sea_rim[1:, :]
    field = with_halo(gradient, (("lon", 2), ("lat", 1)), rim_width)
    for step_number in range(PASSES):
        high, wide = field.shape[1], field.shape[2]
        field = one_pass(
            field,
            east_face[step_number : step_number + high, step_number : step_number + wide - 1],
            north_face[step_number : step_number + high - 1, step_number : step_number + wide],
        )
    gradient = field
    return gradient


def solution(mesh):
    placed = (
        P(None, "lat", "lon"),
        P("lat", "lon"),
        P("lat", "lon"),
        P("lat", "lon"),
        P("lat", "lon"),
        P("lat", "lon"),
        P(None, "lat", "lon"),
        P(None, "lat", "lon"),
    )
    return jax.shard_map(
        body, mesh=mesh, in_specs=placed, out_specs=P(None, "lat", "lon"), check_vma=False
    )
```

```python
import jax
import jax.numpy as jnp
from jax import lax
from jax.sharding import PartitionSpec as P

PASSES = 8


def with_halo(block, sides, width):
    for axis, dim in sides:
        count = lax.axis_size(axis)
        forward = [(i, i + 1) for i in range(count - 1)]
        forward.append((count - 1, 0))
        backward = [(target, source) for source, target in forward]
        low = lax.ppermute(
            lax.slice_in_dim(block, block.shape[dim] - width, None, axis=dim), axis, forward
        )
        high = lax.ppermute(lax.slice_in_dim(block, 0, width, axis=dim), axis, backward)
        block = jnp.concatenate([low, block, high], axis=dim)
    return block


def one_pass(layer_field, east_face, north_face):
    flux_east = east_face * (layer_field[:, :, 1:] - layer_field[:, :, :-1])
    flux_north = north_face * (layer_field[:, 1:, :] - layer_field[:, :-1, :])
    return (
        layer_field[:, 1:-1, 1:-1]
        + flux_east[:, 1:-1, 1:]
        - flux_east[:, 1:-1, :-1]
        + flux_north[:, 1:, 1:-1]
        - flux_north[:, :-1, 1:-1]
    )


def body(state, coef_lon, coef_lat, land_sea, send_cols, send_count, obs_value, obs_weight):
    levels, rows_here, cols_here = state.shape
    lon_count = lax.axis_size("lon")
    lat_count = lax.axis_size("lat")
    slots = send_cols.shape[1]
    capacity = slots // lon_count
    columns = state.reshape(levels, rows_here * cols_here)
    targets = send_cols[0]
    slot_index = jnp.arange(slots, dtype=jnp.int32)
    limits = jnp.broadcast_to(send_count[0][:, None], (lon_count, capacity)).reshape(slots)
    usable = jnp.where(slot_index % capacity < limits, 1.0, 0.0).astype(jnp.float32)
    held = jnp.stack([obs_value[:, 0, :], obs_weight[:, 0, :]])
    at_owner = lax.all_to_all(held, "lon", split_axis=2, concat_axis=2, tiled=True)
    at_column = jnp.take(columns, targets, axis=1)
    weighted = at_owner[1] * (at_owner[0] - at_column) * usable
    sea = land_sea.astype(jnp.float32)
    gradient = jnp.zeros((levels, rows_here * cols_here), jnp.float32).at[:, targets].add(weighted)
    gradient = gradient.reshape(levels, rows_here, cols_here) * sea[None]
    rim_width = PASSES
    stacked = jnp.stack([sea, coef_lon, coef_lat])
    padded = with_halo(stacked, (("lon", 2), ("lat", 1)), rim_width)
    lat_index = lax.axis_index("lat")
    row_place = jnp.arange(rows_here + 2 * rim_width, dtype=jnp.int32)
    outside = (row_place < rim_width) & (lat_index == 0) | (row_place >= rows_here + rim_width) & (
        lat_index == lat_count - 1
    )
    inside = jnp.where(outside, 0.0, 1.0).astype(jnp.float32)[:, None]
    sea_rim = padded[0] * inside
    east_face = padded[1][:, :-1] * sea_rim[:, :-1] * sea_rim[:, 1:]
    north_face = padded[2][:-1, :] * sea_rim[:-1, :] * sea_rim[1:, :]
    field = with_halo(gradient, (("lon", 2), ("lat", 1)), rim_width)
    for step_number in range(PASSES):
        high, wide = field.shape[1], field.shape[2]
        field = one_pass(
            field,
            east_face[step_number : step_number + high, step_number : step_number + wide - 1],
            north_face[step_number : step_number + high - 1, step_number : step_number + wide],
        )
    gradient = field
    return gradient


def solution(mesh):
    placed = (
        P(None, "lat", "lon"),
        P("lat", "lon"),
        P("lat", "lon"),
        P("lat", "lon"),
        P("lat", "lon"),
        P("lat", "lon"),
        P(None, "lat", "lon"),
        P(None, "lat", "lon"),
    )
    return jax.shard_map(
        body, mesh=mesh, in_specs=placed, out_specs=P(None, "lat", "lon"), check_vma=False
    )
```

```python
import jax
import jax.numpy as jnp
from jax import lax
from jax.sharding import PartitionSpec as P

PASSES = 8


def with_halo(block, sides, width):
    for axis, dim in sides:
        count = lax.axis_size(axis)
        forward = [(i, i + 1) for i in range(count - 1)]
        forward.append((count - 1, 0))
        backward = [(target, source) for source, target in forward]
        low = lax.ppermute(
            lax.slice_in_dim(block, block.shape[dim] - width, None, axis=dim), axis, forward
        )
        high = lax.ppermute(lax.slice_in_dim(block, 0, width, axis=dim), axis, backward)
        block = jnp.concatenate([low, block, high], axis=dim)
    return block


def one_pass(layer_field, east_face, north_face):
    flux_east = east_face * (layer_field[:, :, 1:] - layer_field[:, :, :-1])
    flux_north = north_face * (layer_field[:, 1:, :] - layer_field[:, :-1, :])
    return (
        layer_field[:, 1:-1, 1:-1]
        + flux_east[:, 1:-1, 1:]
        - flux_east[:, 1:-1, :-1]
        + flux_north[:, 1:, 1:-1]
        - flux_north[:, :-1, 1:-1]
    )


def body(state, coef_lon, coef_lat, land_sea, send_cols, send_count, obs_value, obs_weight):
    levels, rows_here, cols_here = state.shape
    lon_count = lax.axis_size("lon")
    lat_count = lax.axis_size("lat")
    slots = send_cols.shape[1]
    capacity = slots // lon_count
    columns = state.reshape(levels, rows_here * cols_here)
    targets = send_cols[0]
    slot_index = jnp.arange(slots, dtype=jnp.int32)
    limits = jnp.broadcast_to(send_count[0][:, None], (lon_count, capacity)).reshape(slots)
    usable = jnp.where(slot_index % capacity < limits, 1.0, 0.0).astype(jnp.float32)
    values = lax.all_to_all(obs_value[:, 0, :], "lon", split_axis=1, concat_axis=1, tiled=True)
    weights = lax.all_to_all(obs_weight[:, 0, :], "lon", split_axis=1, concat_axis=1, tiled=True)
    at_column = jnp.take(columns, targets, axis=1)
    weighted = lax.optimization_barrier(weights * (values - at_column) * usable)
    sea = land_sea.astype(jnp.float32)
    gradient = jnp.zeros((levels, rows_here * cols_here), jnp.float32).at[:, targets].add(weighted)
    gradient = gradient.reshape(levels, rows_here, cols_here) * sea[None]
    rim_width = PASSES
    stacked = jnp.stack([sea, coef_lon, coef_lat])
    padded = with_halo(stacked, (("lon", 2), ("lat", 1)), rim_width)
    lat_index = lax.axis_index("lat")
    row_place = jnp.arange(rows_here + 2 * rim_width, dtype=jnp.int32)
    outside = (row_place < rim_width) & (lat_index == 0) | (row_place >= rows_here + rim_width) & (
        lat_index == lat_count - 1
    )
    inside = jnp.where(outside, 0.0, 1.0).astype(jnp.float32)[:, None]
    sea_rim = padded[0] * inside
    east_face = padded[1][:, :-1] * sea_rim[:, :-1] * sea_rim[:, 1:]
    north_face = padded[2][:-1, :] * sea_rim[:-1, :] * sea_rim[1:, :]
    field = with_halo(gradient, (("lon", 2), ("lat", 1)), rim_width)
    for step_number in range(PASSES):
        high, wide = field.shape[1], field.shape[2]
        field = one_pass(
            field,
            east_face[step_number : step_number + high, step_number : step_number + wide - 1],
            north_face[step_number : step_number + high - 1, step_number : step_number + wide],
        )
    gradient = field
    return gradient


def solution(mesh):
    placed = (
        P(None, "lat", "lon"),
        P("lat", "lon"),
        P("lat", "lon"),
        P("lat", "lon"),
        P("lat", "lon"),
        P("lat", "lon"),
        P(None, "lat", "lon"),
        P(None, "lat", "lon"),
    )
    return jax.shard_map(
        body, mesh=mesh, in_specs=placed, out_specs=P(None, "lat", "lon"), check_vma=False
    )
```

```python
import jax
import jax.numpy as jnp
from jax import lax
from jax.sharding import PartitionSpec as P

PASSES = 8


def with_halo(block, sides, width):
    for axis, dim in sides:
        count = lax.axis_size(axis)
        forward = [(i, i + 1) for i in range(count - 1)]
        forward.append((count - 1, 0))
        backward = [(target, source) for source, target in forward]
        low = lax.ppermute(
            lax.slice_in_dim(block, block.shape[dim] - width, None, axis=dim), axis, forward
        )
        high = lax.ppermute(lax.slice_in_dim(block, 0, width, axis=dim), axis, backward)
        block = jnp.concatenate([low, block, high], axis=dim)
    return block


def one_pass(layer_field, east_face, north_face):
    flux_east = east_face * (layer_field[:, :, 1:] - layer_field[:, :, :-1])
    flux_north = north_face * (layer_field[:, 1:, :] - layer_field[:, :-1, :])
    return (
        layer_field[:, 1:-1, 1:-1]
        + flux_east[:, 1:-1, 1:]
        - flux_east[:, 1:-1, :-1]
        + flux_north[:, 1:, 1:-1]
        - flux_north[:, :-1, 1:-1]
    )


def body(state, coef_lon, coef_lat, land_sea, send_cols, send_count, obs_value, obs_weight):
    levels, rows_here, cols_here = state.shape
    lon_count = lax.axis_size("lon")
    lat_count = lax.axis_size("lat")
    slots = send_cols.shape[1]
    capacity = slots // lon_count
    columns = state.reshape(levels, rows_here * cols_here)
    targets = send_cols[0]
    slot_index = jnp.arange(slots, dtype=jnp.int32)
    limits = jnp.broadcast_to(send_count[0][:, None], (lon_count, capacity)).reshape(slots)
    usable = jnp.where(slot_index % capacity < limits, 1.0, 0.0).astype(jnp.float32)
    chunked = (levels, lon_count, capacity)
    held = jnp.concatenate(
        [obs_value[:, 0, :].reshape(chunked), obs_weight[:, 0, :].reshape(chunked)], axis=2
    ).reshape(levels, 2 * slots)
    at_owner = lax.all_to_all(held, "lon", split_axis=1, concat_axis=1, tiled=True)
    at_owner = at_owner.reshape(levels, lon_count, 2 * capacity)
    values = at_owner[:, :, :capacity].reshape(levels, slots)
    weights = at_owner[:, :, capacity:].reshape(levels, slots)
    at_column = jnp.take(columns, targets, axis=1)
    weighted = lax.optimization_barrier(weights * (values - at_column) * usable)
    sea = land_sea.astype(jnp.float32)
    gradient = jnp.zeros((levels, rows_here * cols_here), jnp.float32).at[:, targets].add(weighted)
    gradient = gradient.reshape(levels, rows_here, cols_here) * sea[None]
    rim_width = PASSES
    stacked = jnp.stack([sea, coef_lon, coef_lat])
    padded = with_halo(stacked, (("lon", 2), ("lat", 1)), rim_width)
    lat_index = lax.axis_index("lat")
    row_place = jnp.arange(rows_here + 2 * rim_width, dtype=jnp.int32)
    outside = (row_place < rim_width) & (lat_index == 0) | (row_place >= rows_here + rim_width) & (
        lat_index == lat_count - 1
    )
    inside = jnp.where(outside, 0.0, 1.0).astype(jnp.float32)[:, None]
    sea_rim = padded[0] * inside
    east_face = padded[1][:, :-1] * sea_rim[:, :-1] * sea_rim[:, 1:]
    north_face = padded[2][:-1, :] * sea_rim[:-1, :] * sea_rim[1:, :]
    field = with_halo(gradient, (("lon", 2), ("lat", 1)), rim_width)
    for step_number in range(PASSES):
        high, wide = field.shape[1], field.shape[2]
        field = one_pass(
            field,
            east_face[step_number : step_number + high, step_number : step_number + wide - 1],
            north_face[step_number : step_number + high - 1, step_number : step_number + wide],
        )
    gradient = field
    return gradient


def solution(mesh):
    placed = (
        P(None, "lat", "lon"),
        P("lat", "lon"),
        P("lat", "lon"),
        P("lat", "lon"),
        P("lat", "lon"),
        P("lat", "lon"),
        P(None, "lat", "lon"),
        P(None, "lat", "lon"),
    )
    return jax.shard_map(
        body, mesh=mesh, in_specs=placed, out_specs=P(None, "lat", "lon"), check_vma=False
    )
```

```python
import jax
import jax.numpy as jnp
from jax import lax
from jax.experimental import pallas as pl
from jax.experimental.pallas import tpu as pltpu
from jax.sharding import PartitionSpec as P

PASSES = 8
CHUNK = 512


def three_parts(x):
    high = x.astype(jnp.bfloat16)
    rest = x - high.astype(jnp.float32)
    middle = rest.astype(jnp.bfloat16)
    low = (rest - middle.astype(jnp.float32)).astype(jnp.bfloat16)
    return high, middle, low


def scatter_kernel(w_ref, rows_ref, cols_ref, out_ref):
    levels, slots = w_ref.shape
    cells, cols_here = out_ref.shape
    rows_here = cells // levels
    out_ref[...] = jnp.zeros_like(out_ref)

    def step(k, carry):
        start = pl.multiple_of(k * CHUNK, CHUNK)
        w = w_ref[:, pl.ds(start, CHUNK)]
        row_hit = lax.broadcasted_iota(jnp.int32, (rows_here, CHUNK), 0) == rows_ref[:, pl.ds(start, CHUNK)]
        col_hit = lax.broadcasted_iota(jnp.int32, (cols_here, CHUNK), 0) == cols_ref[:, pl.ds(start, CHUNK)]
        col_hit = col_hit.astype(jnp.float32).astype(jnp.bfloat16)
        for part in three_parts(w):
            spread = jnp.where(row_hit[None], part.astype(jnp.float32)[:, None, :], 0.0)
            spread = spread.reshape(cells, CHUNK).astype(jnp.bfloat16)
            out_ref[...] += lax.dot_general(
                spread, col_hit, (((1,), (1,)), ((), ())), preferred_element_type=jnp.float32
            )
        return carry

    lax.fori_loop(0, slots // CHUNK, step, 0)


def gather_kernel(state_ref, rows_ref, cols_ref, out_ref):
    levels, slots = out_ref.shape
    cells, cols_here = state_ref.shape
    rows_here = cells // levels
    parts = three_parts(state_ref[...])

    def step(k, carry):
        start = pl.multiple_of(k * CHUNK, CHUNK)
        col_hit = lax.broadcasted_iota(jnp.int32, (cols_here, CHUNK), 0) == cols_ref[:, pl.ds(start, CHUNK)]
        col_hit = col_hit.astype(jnp.float32).astype(jnp.bfloat16)
        picked = None
        for part in parts:
            term = jnp.dot(part, col_hit, preferred_element_type=jnp.float32)
            picked = term if picked is None else picked + term
        row_hit = lax.broadcasted_iota(jnp.int32, (rows_here, CHUNK), 0) == rows_ref[:, pl.ds(start, CHUNK)]
        chosen = jnp.where(row_hit[None], picked.reshape(levels, rows_here, CHUNK), 0.0)
        out_ref[:, pl.ds(start, CHUNK)] = jnp.sum(chosen, axis=1)
        return carry

    lax.fori_loop(0, slots // CHUNK, step, 0)


def vmem_call(kernel, out_shape, flops, nbytes):
    return pl.pallas_call(
        kernel,
        out_shape=out_shape,
        in_specs=[pl.BlockSpec(memory_space=pltpu.VMEM)] * 3,
        out_specs=pl.BlockSpec(memory_space=pltpu.VMEM),
        cost_estimate=pl.CostEstimate(flops=flops, bytes_accessed=nbytes, transcendentals=0),
    )


def onehot_scatter(w, rows, cols, rows_here, cols_here):
    levels, slots = w.shape
    shape = jax.ShapeDtypeStruct((levels * rows_here, cols_here), jnp.float32)
    flops = 6 * levels * rows_here * cols_here * slots
    return vmem_call(scatter_kernel, shape, flops, 4 * (levels * slots + 2 * slots + levels * rows_here * cols_here))(w, rows, cols)


def onehot_gather(state2d, rows, cols, levels):
    cells, cols_here = state2d.shape
    slots = rows.shape[1]
    shape = jax.ShapeDtypeStruct((levels, slots), jnp.float32)
    flops = 6 * cells * cols_here * slots
    return vmem_call(gather_kernel, shape, flops, 4 * (levels * slots + 2 * slots + cells * cols_here))(state2d, rows, cols)


def with_halo(block, sides, width):
    for axis, dim in sides:
        count = lax.axis_size(axis)
        forward = [(i, i + 1) for i in range(count - 1)]
        forward.append((count - 1, 0))
        backward = [(target, source) for source, target in forward]
        low = lax.ppermute(
            lax.slice_in_dim(block, block.shape[dim] - width, None, axis=dim), axis, forward
        )
        high = lax.ppermute(lax.slice_in_dim(block, 0, width, axis=dim), axis, backward)
        block = jnp.concatenate([low, block, high], axis=dim)
    return block


def one_pass(layer_field, east_face, north_face):
    flux_east = east_face * (layer_field[:, :, 1:] - layer_field[:, :, :-1])
    flux_north = north_face * (layer_field[:, 1:, :] - layer_field[:, :-1, :])
    return (
        layer_field[:, 1:-1, 1:-1]
        + flux_east[:, 1:-1, 1:]
        - flux_east[:, 1:-1, :-1]
        + flux_north[:, 1:, 1:-1]
        - flux_north[:, :-1, 1:-1]
    )


def body(state, coef_lon, coef_lat, land_sea, send_cols, send_count, obs_value, obs_weight):
    levels, rows_here, cols_here = state.shape
    lon_count = lax.axis_size("lon")
    lat_count = lax.axis_size("lat")
    slots = send_cols.shape[1]
    capacity = slots // lon_count
    targets = send_cols[0]
    slot_index = jnp.arange(slots, dtype=jnp.int32)
    limits = jnp.broadcast_to(send_count[0][:, None], (lon_count, capacity)).reshape(slots)
    usable = jnp.where(slot_index % capacity < limits, 1.0, 0.0).astype(jnp.float32)
    chunked = (levels, lon_count, capacity)
    held = jnp.concatenate(
        [obs_value[:, 0, :].reshape(chunked), obs_weight[:, 0, :].reshape(chunked)], axis=2
    ).reshape(levels, 2 * slots)
    at_owner = lax.all_to_all(held, "lon", split_axis=1, concat_axis=1, tiled=True)
    at_owner = at_owner.reshape(levels, lon_count, 2 * capacity)
    values = at_owner[:, :, :capacity].reshape(levels, slots)
    weights = at_owner[:, :, capacity:].reshape(levels, slots)
    target_rows = (targets // cols_here)[None, :]
    target_cols = (targets % cols_here)[None, :]
    at_column = onehot_gather(state.reshape(levels * rows_here, cols_here), target_rows, target_cols, levels)
    weighted = weights * (values - at_column) * usable
    sea = land_sea.astype(jnp.float32)
    gradient = onehot_scatter(weighted, target_rows, target_cols, rows_here, cols_here)
    gradient = gradient.reshape(levels, rows_here, cols_here) * sea[None]
    rim_width = PASSES
    stacked = jnp.stack([sea, coef_lon, coef_lat])
    padded = with_halo(stacked, (("lon", 2), ("lat", 1)), rim_width)
    lat_index = lax.axis_index("lat")
    row_place = jnp.arange(rows_here + 2 * rim_width, dtype=jnp.int32)
    outside = (row_place < rim_width) & (lat_index == 0) | (row_place >= rows_here + rim_width) & (
        lat_index == lat_count - 1
    )
    inside = jnp.where(outside, 0.0, 1.0).astype(jnp.float32)[:, None]
    sea_rim = padded[0] * inside
    east_face = padded[1][:, :-1] * sea_rim[:, :-1] * sea_rim[:, 1:]
    north_face = padded[2][:-1, :] * sea_rim[:-1, :] * sea_rim[1:, :]
    field = with_halo(gradient, (("lon", 2), ("lat", 1)), rim_width)
    for step_number in range(PASSES):
        high, wide = field.shape[1], field.shape[2]
        field = one_pass(
            field,
            east_face[step_number : step_number + high, step_number : step_number + wide - 1],
            north_face[step_number : step_number + high - 1, step_number : step_number + wide],
        )
    gradient = field
    return gradient


def solution(mesh):
    placed = (
        P(None, "lat", "lon"),
        P("lat", "lon"),
        P("lat", "lon"),
        P("lat", "lon"),
        P("lat", "lon"),
        P("lat", "lon"),
        P(None, "lat", "lon"),
        P(None, "lat", "lon"),
    )
    return jax.shard_map(
        body, mesh=mesh, in_specs=placed, out_specs=P(None, "lat", "lon"), check_vma=False
    )
```

```python
import jax
import jax.numpy as jnp
from jax import lax
from jax.experimental import pallas as pl
from jax.experimental.pallas import tpu as pltpu
from jax.sharding import PartitionSpec as P

PASSES = 8
CHUNK = 512


def three_parts(x):
    high = x.astype(jnp.bfloat16)
    rest = x - high.astype(jnp.float32)
    middle = rest.astype(jnp.bfloat16)
    low = (rest - middle.astype(jnp.float32)).astype(jnp.bfloat16)
    return high, middle, low


def scatter_kernel(w_ref, rows_ref, cols_ref, out_ref):
    levels, slots = w_ref.shape
    cells, cols_here = out_ref.shape
    rows_here = cells // levels
    out_ref[...] = jnp.zeros_like(out_ref)

    def step(k, carry):
        start = pl.multiple_of(k * CHUNK, CHUNK)
        w = w_ref[:, pl.ds(start, CHUNK)]
        row_hit = lax.broadcasted_iota(jnp.int32, (rows_here, CHUNK), 0) == rows_ref[:, pl.ds(start, CHUNK)]
        col_hit = lax.broadcasted_iota(jnp.int32, (cols_here, CHUNK), 0) == cols_ref[:, pl.ds(start, CHUNK)]
        col_hit = col_hit.astype(jnp.float32).astype(jnp.bfloat16)
        for part in three_parts(w):
            spread = jnp.where(row_hit[None], part.astype(jnp.float32)[:, None, :], 0.0)
            spread = spread.reshape(cells, CHUNK).astype(jnp.bfloat16)
            out_ref[...] += lax.dot_general(
                spread, col_hit, (((1,), (1,)), ((), ())), preferred_element_type=jnp.float32
            )
        return carry

    lax.fori_loop(0, slots // CHUNK, step, 0)


def gather_kernel(state_ref, rows_ref, cols_ref, out_ref):
    levels, slots = out_ref.shape
    cells, cols_here = state_ref.shape
    rows_here = cells // levels
    parts = three_parts(state_ref[...])

    def step(k, carry):
        start = pl.multiple_of(k * CHUNK, CHUNK)
        col_hit = lax.broadcasted_iota(jnp.int32, (cols_here, CHUNK), 0) == cols_ref[:, pl.ds(start, CHUNK)]
        col_hit = col_hit.astype(jnp.float32).astype(jnp.bfloat16)
        picked = None
        for part in parts:
            term = jnp.dot(part, col_hit, preferred_element_type=jnp.float32)
            picked = term if picked is None else picked + term
        row_hit = lax.broadcasted_iota(jnp.int32, (rows_here, CHUNK), 0) == rows_ref[:, pl.ds(start, CHUNK)]
        chosen = jnp.where(row_hit[None], picked.reshape(levels, rows_here, CHUNK), 0.0)
        out_ref[:, pl.ds(start, CHUNK)] = jnp.sum(chosen, axis=1)
        return carry

    lax.fori_loop(0, slots // CHUNK, step, 0)


def vmem_call(kernel, out_shape, flops, nbytes):
    return pl.pallas_call(
        kernel,
        out_shape=out_shape,
        in_specs=[pl.BlockSpec(memory_space=pltpu.VMEM)] * 3,
        out_specs=pl.BlockSpec(memory_space=pltpu.VMEM),
        cost_estimate=pl.CostEstimate(flops=flops, bytes_accessed=nbytes, transcendentals=0),
    )


def onehot_scatter(w, rows, cols, rows_here, cols_here):
    levels, slots = w.shape
    shape = jax.ShapeDtypeStruct((levels * rows_here, cols_here), jnp.float32)
    flops = 6 * levels * rows_here * cols_here * slots
    return vmem_call(scatter_kernel, shape, flops, 4 * (levels * slots + 2 * slots + levels * rows_here * cols_here))(w, rows, cols)


def onehot_gather(state2d, rows, cols, levels):
    cells, cols_here = state2d.shape
    slots = rows.shape[1]
    shape = jax.ShapeDtypeStruct((levels, slots), jnp.float32)
    flops = 6 * cells * cols_here * slots
    return vmem_call(gather_kernel, shape, flops, 4 * (levels * slots + 2 * slots + cells * cols_here))(state2d, rows, cols)


def with_halo(block, sides, width):
    for axis, dim in sides:
        count = lax.axis_size(axis)
        forward = [(i, i + 1) for i in range(count - 1)]
        forward.append((count - 1, 0))
        backward = [(target, source) for source, target in forward]
        low = lax.ppermute(
            lax.slice_in_dim(block, block.shape[dim] - width, None, axis=dim), axis, forward
        )
        high = lax.ppermute(lax.slice_in_dim(block, 0, width, axis=dim), axis, backward)
        block = jnp.concatenate([low, block, high], axis=dim)
    return block


def one_pass(layer_field, east_face, north_face):
    flux_east = east_face * (layer_field[:, :, 1:] - layer_field[:, :, :-1])
    flux_north = north_face * (layer_field[:, 1:, :] - layer_field[:, :-1, :])
    return (
        layer_field[:, 1:-1, 1:-1]
        + flux_east[:, 1:-1, 1:]
        - flux_east[:, 1:-1, :-1]
        + flux_north[:, 1:, 1:-1]
        - flux_north[:, :-1, 1:-1]
    )


def body(state, coef_lon, coef_lat, land_sea, send_cols, send_count, obs_value, obs_weight):
    levels, rows_here, cols_here = state.shape
    lon_count = lax.axis_size("lon")
    lat_count = lax.axis_size("lat")
    slots = send_cols.shape[1]
    capacity = slots // lon_count
    targets = send_cols[0]
    slot_index = jnp.arange(slots, dtype=jnp.int32)
    limits = jnp.broadcast_to(send_count[0][:, None], (lon_count, capacity)).reshape(slots)
    usable = jnp.where(slot_index % capacity < limits, 1.0, 0.0).astype(jnp.float32)
    chunked = (levels, lon_count, capacity)
    held = jnp.concatenate(
        [obs_value[:, 0, :].reshape(chunked), obs_weight[:, 0, :].reshape(chunked)], axis=2
    ).reshape(levels, 2 * slots)
    at_owner = lax.all_to_all(held, "lon", split_axis=1, concat_axis=1, tiled=True)
    at_owner = at_owner.reshape(levels, lon_count, 2 * capacity)
    values = at_owner[:, :, :capacity].reshape(levels, slots)
    weights = at_owner[:, :, capacity:].reshape(levels, slots)
    target_rows = (targets // cols_here)[None, :]
    target_cols = (targets % cols_here)[None, :]
    at_column = onehot_gather(state.reshape(levels * rows_here, cols_here), target_rows, target_cols, levels)
    weighted = weights * (values - at_column) * usable
    sea = land_sea.astype(jnp.float32)
    gradient = onehot_scatter(weighted, target_rows, target_cols, rows_here, cols_here)
    gradient = gradient.reshape(levels, rows_here, cols_here) * sea[None]
    rim_width = PASSES
    stacked = jnp.concatenate([gradient, sea[None], coef_lon[None], coef_lat[None]], axis=0)
    padded = with_halo(stacked, (("lon", 2), ("lat", 1)), rim_width)
    field = padded[:levels]
    padded = padded[levels:]
    lat_index = lax.axis_index("lat")
    row_place = jnp.arange(rows_here + 2 * rim_width, dtype=jnp.int32)
    outside = (row_place < rim_width) & (lat_index == 0) | (row_place >= rows_here + rim_width) & (
        lat_index == lat_count - 1
    )
    inside = jnp.where(outside, 0.0, 1.0).astype(jnp.float32)[:, None]
    sea_rim = padded[0] * inside
    east_face = padded[1][:, :-1] * sea_rim[:, :-1] * sea_rim[:, 1:]
    north_face = padded[2][:-1, :] * sea_rim[:-1, :] * sea_rim[1:, :]
    for step_number in range(PASSES):
        high, wide = field.shape[1], field.shape[2]
        field = one_pass(
            field,
            east_face[step_number : step_number + high, step_number : step_number + wide - 1],
            north_face[step_number : step_number + high - 1, step_number : step_number + wide],
        )
    gradient = field
    return gradient


def solution(mesh):
    placed = (
        P(None, "lat", "lon"),
        P("lat", "lon"),
        P("lat", "lon"),
        P("lat", "lon"),
        P("lat", "lon"),
        P("lat", "lon"),
        P(None, "lat", "lon"),
        P(None, "lat", "lon"),
    )
    return jax.shard_map(
        body, mesh=mesh, in_specs=placed, out_specs=P(None, "lat", "lon"), check_vma=False
    )
```

```python
import jax
import jax.numpy as jnp
from jax import lax
from jax.experimental import pallas as pl
from jax.experimental.pallas import tpu as pltpu
from jax.sharding import PartitionSpec as P

PASSES = 8
CHUNK = 512


def three_parts(x):
    high = x.astype(jnp.bfloat16)
    rest = x - high.astype(jnp.float32)
    middle = rest.astype(jnp.bfloat16)
    low = (rest - middle.astype(jnp.float32)).astype(jnp.bfloat16)
    return high, middle, low


def scatter_kernel(w_ref, rows_ref, cols_ref, out_ref):
    levels, slots = w_ref.shape
    cells, cols_here = out_ref.shape
    rows_here = cells // levels
    out_ref[...] = jnp.zeros_like(out_ref)

    def step(k, carry):
        start = pl.multiple_of(k * CHUNK, CHUNK)
        w = w_ref[:, pl.ds(start, CHUNK)]
        row_hit = lax.broadcasted_iota(jnp.int32, (rows_here, CHUNK), 0) == rows_ref[:, pl.ds(start, CHUNK)]
        col_hit = lax.broadcasted_iota(jnp.int32, (cols_here, CHUNK), 0) == cols_ref[:, pl.ds(start, CHUNK)]
        col_hit = col_hit.astype(jnp.float32).astype(jnp.bfloat16)
        for part in three_parts(w):
            spread = jnp.where(row_hit[None], part.astype(jnp.float32)[:, None, :], 0.0)
            spread = spread.reshape(cells, CHUNK).astype(jnp.bfloat16)
            out_ref[...] += lax.dot_general(
                spread, col_hit, (((1,), (1,)), ((), ())), preferred_element_type=jnp.float32
            )
        return carry

    lax.fori_loop(0, slots // CHUNK, step, 0)


def gather_kernel(state_ref, rows_ref, cols_ref, out_ref):
    levels, slots = out_ref.shape
    cells, cols_here = state_ref.shape
    rows_here = cells // levels
    parts = three_parts(state_ref[...])

    def step(k, carry):
        start = pl.multiple_of(k * CHUNK, CHUNK)
        col_hit = lax.broadcasted_iota(jnp.int32, (cols_here, CHUNK), 0) == cols_ref[:, pl.ds(start, CHUNK)]
        col_hit = col_hit.astype(jnp.float32).astype(jnp.bfloat16)
        picked = None
        for part in parts:
            term = jnp.dot(part, col_hit, preferred_element_type=jnp.float32)
            picked = term if picked is None else picked + term
        row_hit = lax.broadcasted_iota(jnp.int32, (rows_here, CHUNK), 0) == rows_ref[:, pl.ds(start, CHUNK)]
        chosen = jnp.where(row_hit[None], picked.reshape(levels, rows_here, CHUNK), 0.0)
        out_ref[:, pl.ds(start, CHUNK)] = jnp.sum(chosen, axis=1)
        return carry

    lax.fori_loop(0, slots // CHUNK, step, 0)


def vmem_call(kernel, out_shape, flops, nbytes):
    return pl.pallas_call(
        kernel,
        out_shape=out_shape,
        in_specs=[pl.BlockSpec(memory_space=pltpu.VMEM)] * 3,
        out_specs=pl.BlockSpec(memory_space=pltpu.VMEM),
        cost_estimate=pl.CostEstimate(flops=flops, bytes_accessed=nbytes, transcendentals=0),
    )


def onehot_scatter(w, rows, cols, rows_here, cols_here):
    levels, slots = w.shape
    shape = jax.ShapeDtypeStruct((levels * rows_here, cols_here), jnp.float32)
    flops = 6 * levels * rows_here * cols_here * slots
    return vmem_call(scatter_kernel, shape, flops, 4 * (levels * slots + 2 * slots + levels * rows_here * cols_here))(w, rows, cols)


def onehot_gather(state2d, rows, cols, levels):
    cells, cols_here = state2d.shape
    slots = rows.shape[1]
    shape = jax.ShapeDtypeStruct((levels, slots), jnp.float32)
    flops = 6 * cells * cols_here * slots
    return vmem_call(gather_kernel, shape, flops, 4 * (levels * slots + 2 * slots + cells * cols_here))(state2d, rows, cols)


def passes_kernel(field_ref, east_ref, north_ref, out_ref):
    levels, rows_out, cols_out = out_ref.shape
    _, high, wide = field_ref.shape
    east = east_ref[...]
    north = north_ref[...]

    def level(l, carry):
        g = field_ref[l]
        for step_number in range(PASSES):
            flux_east = east * (pltpu.roll(g, wide - 1, 1) - g)
            flux_north = north * (pltpu.roll(g, high - 1, 0) - g)
            g = g + flux_east - pltpu.roll(flux_east, 1, 1) + flux_north - pltpu.roll(flux_north, 1, 0)
        out_ref[l] = g[:rows_out, :cols_out]
        return carry

    lax.fori_loop(0, levels, level, 0)


def diffuse(field, east, north, rows_out, cols_out):
    levels, high, wide = field.shape
    return pl.pallas_call(
        passes_kernel,
        out_shape=jax.ShapeDtypeStruct((levels, rows_out, cols_out), jnp.float32),
        in_specs=[pl.BlockSpec(memory_space=pltpu.VMEM)] * 3,
        out_specs=pl.BlockSpec(memory_space=pltpu.VMEM),
        cost_estimate=pl.CostEstimate(
            flops=10 * PASSES * levels * high * wide, bytes_accessed=4 * levels * (high * wide + rows_out * cols_out),
            transcendentals=0,
        ),
    )(field, east, north)


def wrapped_halo(block, width, extent):
    lon_count = lax.axis_size("lon")
    lat_count = lax.axis_size("lat")
    lon_up = [(i, (i + 1) % lon_count) for i in range(lon_count)]
    lon_down = [(j, i) for i, j in lon_up]
    lat_up = [(i, (i + 1) % lat_count) for i in range(lat_count)]
    lat_down = [(j, i) for i, j in lat_up]
    west = lax.ppermute(block[..., -width:], "lon", lon_up)
    east = lax.ppermute(block[..., :width], "lon", lon_down)
    gap = jnp.zeros(block.shape[:-1] + (extent - block.shape[-1] - 2 * width,), block.dtype)
    block = jnp.concatenate([block, east, gap, west], axis=-1)
    south = lax.ppermute(block[..., -width:, :], "lat", lat_up)
    north = lax.ppermute(block[..., :width, :], "lat", lat_down)
    return jnp.concatenate([block, north, south], axis=-2)


def body(state, coef_lon, coef_lat, land_sea, send_cols, send_count, obs_value, obs_weight):
    levels, rows_here, cols_here = state.shape
    lon_count = lax.axis_size("lon")
    lat_count = lax.axis_size("lat")
    slots = send_cols.shape[1]
    capacity = slots // lon_count
    targets = send_cols[0]
    slot_index = jnp.arange(slots, dtype=jnp.int32)
    limits = jnp.broadcast_to(send_count[0][:, None], (lon_count, capacity)).reshape(slots)
    usable = jnp.where(slot_index % capacity < limits, 1.0, 0.0).astype(jnp.float32)
    chunked = (levels, lon_count, capacity)
    held = jnp.concatenate(
        [obs_value[:, 0, :].reshape(chunked), obs_weight[:, 0, :].reshape(chunked)], axis=2
    ).reshape(levels, 2 * slots)
    at_owner = lax.all_to_all(held, "lon", split_axis=1, concat_axis=1, tiled=True)
    at_owner = at_owner.reshape(levels, lon_count, 2 * capacity)
    values = at_owner[:, :, :capacity].reshape(levels, slots)
    weights = at_owner[:, :, capacity:].reshape(levels, slots)
    target_rows = (targets // cols_here)[None, :]
    target_cols = (targets % cols_here)[None, :]
    at_column = onehot_gather(state.reshape(levels * rows_here, cols_here), target_rows, target_cols, levels)
    weighted = weights * (values - at_column) * usable
    sea = land_sea.astype(jnp.float32)
    gradient = onehot_scatter(weighted, target_rows, target_cols, rows_here, cols_here)
    gradient = gradient.reshape(levels, rows_here, cols_here) * sea[None]
    rim_width = PASSES
    lanes_out = 128 * ((cols_here + 2 * rim_width + 127) // 128)
    stacked = jnp.concatenate([gradient, sea[None], coef_lon[None], coef_lat[None]], axis=0)
    padded = wrapped_halo(stacked, rim_width, lanes_out)
    lat_index = lax.axis_index("lat")
    row_place = jnp.arange(rows_here + 2 * rim_width, dtype=jnp.int32)
    outside = (row_place >= rows_here + rim_width) & (lat_index == 0) | (
        row_place >= rows_here
    ) & (row_place < rows_here + rim_width) & (lat_index == lat_count - 1)
    inside = jnp.where(outside, 0.0, 1.0).astype(jnp.float32)[:, None]
    sea_rim = padded[levels] * inside
    east_face = padded[levels + 1] * sea_rim * jnp.roll(sea_rim, -1, axis=1)
    north_face = padded[levels + 2] * sea_rim * jnp.roll(sea_rim, -1, axis=0)
    gradient = diffuse(padded[:levels], east_face, north_face, rows_here, cols_here)
    return gradient


def solution(mesh):
    placed = (
        P(None, "lat", "lon"),
        P("lat", "lon"),
        P("lat", "lon"),
        P("lat", "lon"),
        P("lat", "lon"),
        P("lat", "lon"),
        P(None, "lat", "lon"),
        P(None, "lat", "lon"),
    )
    return jax.shard_map(
        body, mesh=mesh, in_specs=placed, out_specs=P(None, "lat", "lon"), check_vma=False
    )
```

```python
import jax
import jax.numpy as jnp
from jax import lax
from jax.experimental import pallas as pl
from jax.experimental.pallas import tpu as pltpu
from jax.sharding import PartitionSpec as P

PASSES = 8
CHUNK = 512


def three_parts(x):
    high = x.astype(jnp.bfloat16)
    rest = x - high.astype(jnp.float32)
    middle = rest.astype(jnp.bfloat16)
    low = (rest - middle.astype(jnp.float32)).astype(jnp.bfloat16)
    return high, middle, low


def scatter_kernel(w_ref, rows_ref, cols_ref, out_ref):
    levels, slots = w_ref.shape
    cells, cols_here = out_ref.shape
    rows_here = cells // levels
    out_ref[...] = jnp.zeros_like(out_ref)

    def step(k, carry):
        start = pl.multiple_of(k * CHUNK, CHUNK)
        w = w_ref[:, pl.ds(start, CHUNK)]
        row_hit = lax.broadcasted_iota(jnp.int32, (rows_here, CHUNK), 0) == rows_ref[:, pl.ds(start, CHUNK)]
        col_hit = lax.broadcasted_iota(jnp.int32, (cols_here, CHUNK), 0) == cols_ref[:, pl.ds(start, CHUNK)]
        col_hit = col_hit.astype(jnp.float32).astype(jnp.bfloat16)
        for part in three_parts(w):
            spread = jnp.where(row_hit[None], part.astype(jnp.float32)[:, None, :], 0.0)
            spread = spread.reshape(cells, CHUNK).astype(jnp.bfloat16)
            out_ref[...] += lax.dot_general(
                spread, col_hit, (((1,), (1,)), ((), ())), preferred_element_type=jnp.float32
            )
        return carry

    lax.fori_loop(0, slots // CHUNK, step, 0)


def gather_kernel(state_ref, rows_ref, cols_ref, out_ref):
    levels, slots = out_ref.shape
    cells, cols_here = state_ref.shape
    rows_here = cells // levels
    parts = three_parts(state_ref[...])

    def step(k, carry):
        start = pl.multiple_of(k * CHUNK, CHUNK)
        col_hit = lax.broadcasted_iota(jnp.int32, (cols_here, CHUNK), 0) == cols_ref[:, pl.ds(start, CHUNK)]
        col_hit = col_hit.astype(jnp.float32).astype(jnp.bfloat16)
        picked = None
        for part in parts:
            term = jnp.dot(part, col_hit, preferred_element_type=jnp.float32)
            picked = term if picked is None else picked + term
        row_hit = lax.broadcasted_iota(jnp.int32, (rows_here, CHUNK), 0) == rows_ref[:, pl.ds(start, CHUNK)]
        chosen = jnp.where(row_hit[None], picked.reshape(levels, rows_here, CHUNK), 0.0)
        out_ref[:, pl.ds(start, CHUNK)] = jnp.sum(chosen, axis=1)
        return carry

    lax.fori_loop(0, slots // CHUNK, step, 0)


def vmem_call(kernel, out_shape, flops, nbytes):
    return pl.pallas_call(
        kernel,
        out_shape=out_shape,
        in_specs=[pl.BlockSpec(memory_space=pltpu.VMEM)] * 3,
        out_specs=pl.BlockSpec(memory_space=pltpu.VMEM),
        cost_estimate=pl.CostEstimate(flops=flops, bytes_accessed=nbytes, transcendentals=0),
    )


def onehot_scatter(w, rows, cols, rows_here, cols_here):
    levels, slots = w.shape
    shape = jax.ShapeDtypeStruct((levels * rows_here, cols_here), jnp.float32)
    flops = 6 * levels * rows_here * cols_here * slots
    return vmem_call(scatter_kernel, shape, flops, 4 * (levels * slots + 2 * slots + levels * rows_here * cols_here))(w, rows, cols)


def onehot_gather(state2d, rows, cols, levels):
    cells, cols_here = state2d.shape
    slots = rows.shape[1]
    shape = jax.ShapeDtypeStruct((levels, slots), jnp.float32)
    flops = 6 * cells * cols_here * slots
    return vmem_call(gather_kernel, shape, flops, 4 * (levels * slots + 2 * slots + cells * cols_here))(state2d, rows, cols)


def with_halo(block, sides, width):
    for axis, dim in sides:
        count = lax.axis_size(axis)
        forward = [(i, i + 1) for i in range(count - 1)]
        forward.append((count - 1, 0))
        backward = [(target, source) for source, target in forward]
        low = lax.slice_in_dim(block, block.shape[dim] - width, None, axis=dim)
        high = lax.slice_in_dim(block, 0, width, axis=dim)
        if dim == block.ndim - 1:
            flat = block.shape[:-2] + (-1,)
            low = lax.ppermute(low.reshape(flat), axis, forward).reshape(low.shape)
            high = lax.ppermute(high.reshape(flat), axis, backward).reshape(high.shape)
        else:
            low = lax.ppermute(low, axis, forward)
            high = lax.ppermute(high, axis, backward)
        block = jnp.concatenate([low, block, high], axis=dim)
    return block


def one_pass(layer_field, east_face, north_face):
    flux_east = east_face * (layer_field[:, :, 1:] - layer_field[:, :, :-1])
    flux_north = north_face * (layer_field[:, 1:, :] - layer_field[:, :-1, :])
    return (
        layer_field[:, 1:-1, 1:-1]
        + flux_east[:, 1:-1, 1:]
        - flux_east[:, 1:-1, :-1]
        + flux_north[:, 1:, 1:-1]
        - flux_north[:, :-1, 1:-1]
    )


def body(state, coef_lon, coef_lat, land_sea, send_cols, send_count, obs_value, obs_weight):
    levels, rows_here, cols_here = state.shape
    lon_count = lax.axis_size("lon")
    lat_count = lax.axis_size("lat")
    slots = send_cols.shape[1]
    capacity = slots // lon_count
    targets = send_cols[0]
    slot_index = jnp.arange(slots, dtype=jnp.int32)
    limits = jnp.broadcast_to(send_count[0][:, None], (lon_count, capacity)).reshape(slots)
    usable = jnp.where(slot_index % capacity < limits, 1.0, 0.0).astype(jnp.float32)
    chunked = (levels, lon_count, capacity)
    held = jnp.concatenate(
        [obs_value[:, 0, :].reshape(chunked), obs_weight[:, 0, :].reshape(chunked)], axis=2
    ).reshape(levels, 2 * slots)
    at_owner = lax.all_to_all(held, "lon", split_axis=1, concat_axis=1, tiled=True)
    at_owner = at_owner.reshape(levels, lon_count, 2 * capacity)
    values = at_owner[:, :, :capacity].reshape(levels, slots)
    weights = at_owner[:, :, capacity:].reshape(levels, slots)
    target_rows = (targets // cols_here)[None, :]
    target_cols = (targets % cols_here)[None, :]
    at_column = onehot_gather(state.reshape(levels * rows_here, cols_here), target_rows, target_cols, levels)
    weighted = weights * (values - at_column) * usable
    sea = land_sea.astype(jnp.float32)
    gradient = onehot_scatter(weighted, target_rows, target_cols, rows_here, cols_here)
    gradient = gradient.reshape(levels, rows_here, cols_here) * sea[None]
    rim_width = PASSES
    stacked = jnp.concatenate([gradient, sea[None], coef_lon[None], coef_lat[None]], axis=0)
    padded = with_halo(stacked, (("lon", 2), ("lat", 1)), rim_width)
    field = padded[:levels]
    padded = padded[levels:]
    lat_index = lax.axis_index("lat")
    row_place = jnp.arange(rows_here + 2 * rim_width, dtype=jnp.int32)
    outside = (row_place < rim_width) & (lat_index == 0) | (row_place >= rows_here + rim_width) & (
        lat_index == lat_count - 1
    )
    inside = jnp.where(outside, 0.0, 1.0).astype(jnp.float32)[:, None]
    sea_rim = padded[0] * inside
    east_face = padded[1][:, :-1] * sea_rim[:, :-1] * sea_rim[:, 1:]
    north_face = padded[2][:-1, :] * sea_rim[:-1, :] * sea_rim[1:, :]
    for step_number in range(PASSES):
        high, wide = field.shape[1], field.shape[2]
        field = one_pass(
            field,
            east_face[step_number : step_number + high, step_number : step_number + wide - 1],
            north_face[step_number : step_number + high - 1, step_number : step_number + wide],
        )
    gradient = field
    return gradient


def solution(mesh):
    placed = (
        P(None, "lat", "lon"),
        P("lat", "lon"),
        P("lat", "lon"),
        P("lat", "lon"),
        P("lat", "lon"),
        P("lat", "lon"),
        P(None, "lat", "lon"),
        P(None, "lat", "lon"),
    )
    return jax.shard_map(
        body, mesh=mesh, in_specs=placed, out_specs=P(None, "lat", "lon"), check_vma=False
    )
```

```python
import jax
import jax.numpy as jnp
from jax import lax
from jax.experimental import pallas as pl
from jax.experimental.pallas import tpu as pltpu
from jax.sharding import PartitionSpec as P

PASSES = 8
CHUNK = 512


def three_parts(x):
    high = x.astype(jnp.bfloat16)
    rest = x - high.astype(jnp.float32)
    middle = rest.astype(jnp.bfloat16)
    low = (rest - middle.astype(jnp.float32)).astype(jnp.bfloat16)
    return high, middle, low


def scatter_kernel(w_ref, rows_ref, cols_ref, out_ref):
    levels, slots = w_ref.shape
    cells, cols_here = out_ref.shape
    rows_here = cells // levels
    out_ref[...] = jnp.zeros_like(out_ref)

    def step(k, carry):
        start = pl.multiple_of(k * CHUNK, CHUNK)
        w = w_ref[:, pl.ds(start, CHUNK)]
        row_hit = lax.broadcasted_iota(jnp.int32, (rows_here, CHUNK), 0) == rows_ref[:, pl.ds(start, CHUNK)]
        col_hit = lax.broadcasted_iota(jnp.int32, (cols_here, CHUNK), 0) == cols_ref[:, pl.ds(start, CHUNK)]
        col_hit = col_hit.astype(jnp.float32).astype(jnp.bfloat16)
        for part in three_parts(w):
            spread = jnp.where(row_hit[None], part.astype(jnp.float32)[:, None, :], 0.0)
            spread = spread.reshape(cells, CHUNK).astype(jnp.bfloat16)
            out_ref[...] += lax.dot_general(
                spread, col_hit, (((1,), (1,)), ((), ())), preferred_element_type=jnp.float32
            )
        return carry

    lax.fori_loop(0, slots // CHUNK, step, 0)


def gather_kernel(state_ref, rows_ref, cols_ref, out_ref):
    levels, slots = out_ref.shape
    cells, cols_here = state_ref.shape
    rows_here = cells // levels
    parts = three_parts(state_ref[...])

    def step(k, carry):
        start = pl.multiple_of(k * CHUNK, CHUNK)
        col_hit = lax.broadcasted_iota(jnp.int32, (cols_here, CHUNK), 0) == cols_ref[:, pl.ds(start, CHUNK)]
        col_hit = col_hit.astype(jnp.float32).astype(jnp.bfloat16)
        picked = None
        for part in parts:
            term = jnp.dot(part, col_hit, preferred_element_type=jnp.float32)
            picked = term if picked is None else picked + term
        row_hit = lax.broadcasted_iota(jnp.int32, (rows_here, CHUNK), 0) == rows_ref[:, pl.ds(start, CHUNK)]
        chosen = jnp.where(row_hit[None], picked.reshape(levels, rows_here, CHUNK), 0.0)
        out_ref[:, pl.ds(start, CHUNK)] = jnp.sum(chosen, axis=1)
        return carry

    lax.fori_loop(0, slots // CHUNK, step, 0)


def vmem_call(kernel, out_shape, flops, nbytes):
    return pl.pallas_call(
        kernel,
        out_shape=out_shape,
        in_specs=[pl.BlockSpec(memory_space=pltpu.VMEM)] * 3,
        out_specs=pl.BlockSpec(memory_space=pltpu.VMEM),
        cost_estimate=pl.CostEstimate(flops=flops, bytes_accessed=nbytes, transcendentals=0),
    )


def onehot_scatter(w, rows, cols, rows_here, cols_here):
    levels, slots = w.shape
    shape = jax.ShapeDtypeStruct((levels * rows_here, cols_here), jnp.float32)
    flops = 6 * levels * rows_here * cols_here * slots
    return vmem_call(scatter_kernel, shape, flops, 4 * (levels * slots + 2 * slots + levels * rows_here * cols_here))(w, rows, cols)


def onehot_gather(state2d, rows, cols, levels):
    cells, cols_here = state2d.shape
    slots = rows.shape[1]
    shape = jax.ShapeDtypeStruct((levels, slots), jnp.float32)
    flops = 6 * cells * cols_here * slots
    return vmem_call(gather_kernel, shape, flops, 4 * (levels * slots + 2 * slots + cells * cols_here))(state2d, rows, cols)


def with_halo(block, sides, width):
    for axis, dim in sides:
        count = lax.axis_size(axis)
        forward = [(i, i + 1) for i in range(count - 1)]
        forward.append((count - 1, 0))
        backward = [(target, source) for source, target in forward]
        low = lax.slice_in_dim(block, block.shape[dim] - width, None, axis=dim)
        high = lax.slice_in_dim(block, 0, width, axis=dim)
        if dim == block.ndim - 1:
            flat = block.shape[:-2] + (-1,)
            low = lax.ppermute(low.reshape(flat), axis, forward).reshape(low.shape)
            high = lax.ppermute(high.reshape(flat), axis, backward).reshape(high.shape)
        else:
            low = lax.ppermute(low, axis, forward)
            high = lax.ppermute(high, axis, backward)
        block = jnp.concatenate([low, block, high], axis=dim)
    return block


def one_pass(field, east_face, north_face, offset):
    high, wide = field.shape[1], field.shape[2]
    rows = slice(offset + 1, offset + high - 1)
    cols = slice(offset + 1, offset + wide - 1)
    centre = field[:, 1:-1, 1:-1]
    east_here = east_face[rows, cols]
    east_west = east_face[rows, offset : offset + wide - 2]
    north_here = north_face[rows, cols]
    north_south = north_face[offset : offset + high - 2, cols]
    return (
        centre
        + east_here * (field[:, 1:-1, 2:] - centre)
        - east_west * (centre - field[:, 1:-1, :-2])
        + north_here * (field[:, 2:, 1:-1] - centre)
        - north_south * (centre - field[:, :-2, 1:-1])
    )


def body(state, coef_lon, coef_lat, land_sea, send_cols, send_count, obs_value, obs_weight):
    levels, rows_here, cols_here = state.shape
    lon_count = lax.axis_size("lon")
    lat_count = lax.axis_size("lat")
    slots = send_cols.shape[1]
    capacity = slots // lon_count
    targets = send_cols[0]
    slot_index = jnp.arange(slots, dtype=jnp.int32)
    limits = jnp.broadcast_to(send_count[0][:, None], (lon_count, capacity)).reshape(slots)
    usable = jnp.where(slot_index % capacity < limits, 1.0, 0.0).astype(jnp.float32)
    chunked = (levels, lon_count, capacity)
    held = jnp.concatenate(
        [obs_value[:, 0, :].reshape(chunked), obs_weight[:, 0, :].reshape(chunked)], axis=2
    ).reshape(levels, 2 * slots)
    at_owner = lax.all_to_all(held, "lon", split_axis=1, concat_axis=1, tiled=True)
    at_owner = at_owner.reshape(levels, lon_count, 2 * capacity)
    values = at_owner[:, :, :capacity].reshape(levels, slots)
    weights = at_owner[:, :, capacity:].reshape(levels, slots)
    target_rows = (targets // cols_here)[None, :]
    target_cols = (targets % cols_here)[None, :]
    at_column = onehot_gather(state.reshape(levels * rows_here, cols_here), target_rows, target_cols, levels)
    weighted = weights * (values - at_column) * usable
    sea = land_sea.astype(jnp.float32)
    gradient = onehot_scatter(weighted, target_rows, target_cols, rows_here, cols_here)
    gradient = gradient.reshape(levels, rows_here, cols_here) * sea[None]
    rim_width = PASSES
    stacked = jnp.concatenate([gradient, sea[None], coef_lon[None], coef_lat[None]], axis=0)
    padded = with_halo(stacked, (("lon", 2), ("lat", 1)), rim_width)
    field = padded[:levels]
    padded = padded[levels:]
    lat_index = lax.axis_index("lat")
    row_place = jnp.arange(rows_here + 2 * rim_width, dtype=jnp.int32)
    outside = (row_place < rim_width) & (lat_index == 0) | (row_place >= rows_here + rim_width) & (
        lat_index == lat_count - 1
    )
    inside = jnp.where(outside, 0.0, 1.0).astype(jnp.float32)[:, None]
    sea_rim = padded[0] * inside
    east_face = padded[1][:, :-1] * sea_rim[:, :-1] * sea_rim[:, 1:]
    north_face = padded[2][:-1, :] * sea_rim[:-1, :] * sea_rim[1:, :]
    for step_number in range(PASSES):
        field = one_pass(field, east_face, north_face, step_number)
    gradient = field
    return gradient


def solution(mesh):
    placed = (
        P(None, "lat", "lon"),
        P("lat", "lon"),
        P("lat", "lon"),
        P("lat", "lon"),
        P("lat", "lon"),
        P("lat", "lon"),
        P(None, "lat", "lon"),
        P(None, "lat", "lon"),
    )
    return jax.shard_map(
        body, mesh=mesh, in_specs=placed, out_specs=P(None, "lat", "lon"), check_vma=False
    )
```

```python
import jax
import jax.numpy as jnp
from jax import lax
from jax.experimental import pallas as pl
from jax.experimental.pallas import tpu as pltpu
from jax.sharding import PartitionSpec as P

PASSES = 8
CHUNK = 512
SCATTER_CHUNK = 1024


def three_parts(x):
    high = x.astype(jnp.bfloat16)
    rest = x - high.astype(jnp.float32)
    middle = rest.astype(jnp.bfloat16)
    low = (rest - middle.astype(jnp.float32)).astype(jnp.bfloat16)
    return high, middle, low


def scatter_kernel(values_ref, weights_ref, seen_ref, usable_ref, rows_ref, cols_ref, sea_ref, out_ref, acc_ref):
    levels, slots = values_ref.shape
    _, rows_here, cols_here = out_ref.shape
    cells = levels * rows_here
    acc_ref[...] = jnp.zeros_like(acc_ref)

    def step(k, carry):
        start = pl.multiple_of(k * SCATTER_CHUNK, SCATTER_CHUNK)
        here = pl.ds(start, SCATTER_CHUNK)
        w = weights_ref[:, here] * (values_ref[:, here] - seen_ref[:, here]) * usable_ref[:, here]
        row_hit = lax.broadcasted_iota(jnp.int32, (rows_here, SCATTER_CHUNK), 0) == rows_ref[:, here]
        col_hit = lax.broadcasted_iota(jnp.int32, (cols_here, SCATTER_CHUNK), 0) == cols_ref[:, here]
        col_hit = col_hit.astype(jnp.float32).astype(jnp.bfloat16)
        spread = [
            jnp.where(row_hit[None], part.astype(jnp.float32)[:, None, :], 0.0)
            .reshape(cells, SCATTER_CHUNK)
            .astype(jnp.bfloat16)
            for part in three_parts(w)
        ]
        acc_ref[...] += lax.dot_general(
            jnp.concatenate(spread, axis=1),
            jnp.concatenate([col_hit] * 3, axis=1),
            (((1,), (1,)), ((), ())),
            preferred_element_type=jnp.float32,
        )
        return carry

    lax.fori_loop(0, slots // SCATTER_CHUNK, step, 0)
    out_ref[...] = acc_ref[...].reshape(levels, rows_here, cols_here) * sea_ref[...][None]


def gather_kernel(state_ref, rows_ref, cols_ref, out_ref):
    levels, slots = out_ref.shape
    cells, cols_here = state_ref.shape
    rows_here = cells // levels
    parts = three_parts(state_ref[...])

    def step(k, carry):
        start = pl.multiple_of(k * CHUNK, CHUNK)
        col_hit = lax.broadcasted_iota(jnp.int32, (cols_here, CHUNK), 0) == cols_ref[:, pl.ds(start, CHUNK)]
        col_hit = col_hit.astype(jnp.float32).astype(jnp.bfloat16)
        picked = None
        for part in parts:
            term = jnp.dot(part, col_hit, preferred_element_type=jnp.float32)
            picked = term if picked is None else picked + term
        row_hit = lax.broadcasted_iota(jnp.int32, (rows_here, CHUNK), 0) == rows_ref[:, pl.ds(start, CHUNK)]
        chosen = jnp.where(row_hit[None], picked.reshape(levels, rows_here, CHUNK), 0.0)
        out_ref[:, pl.ds(start, CHUNK)] = jnp.sum(chosen, axis=1)
        return carry

    lax.fori_loop(0, slots // CHUNK, step, 0)


def vmem_call(kernel, out_shape, flops, nbytes):
    return pl.pallas_call(
        kernel,
        out_shape=out_shape,
        in_specs=[pl.BlockSpec(memory_space=pltpu.VMEM)] * 3,
        out_specs=pl.BlockSpec(memory_space=pltpu.VMEM),
        cost_estimate=pl.CostEstimate(flops=flops, bytes_accessed=nbytes, transcendentals=0),
    )


def onehot_scatter(values, weights, seen, usable, rows, cols, sea):
    levels, slots = values.shape
    rows_here, cols_here = sea.shape
    shape = jax.ShapeDtypeStruct((levels, rows_here, cols_here), jnp.float32)
    flops = 6 * levels * rows_here * cols_here * slots
    return pl.pallas_call(
        scatter_kernel,
        out_shape=shape,
        in_specs=[pl.BlockSpec(memory_space=pltpu.VMEM)] * 7,
        out_specs=pl.BlockSpec(memory_space=pltpu.VMEM),
        scratch_shapes=[pltpu.VMEM((levels * rows_here, cols_here), jnp.float32)],
        cost_estimate=pl.CostEstimate(
            flops=flops, bytes_accessed=4 * (3 * levels * slots + 3 * slots + levels * rows_here * cols_here),
            transcendentals=0,
        ),
    )(values, weights, seen, usable, rows, cols, sea)


def onehot_gather(state2d, rows, cols, levels):
    cells, cols_here = state2d.shape
    slots = rows.shape[1]
    shape = jax.ShapeDtypeStruct((levels, slots), jnp.float32)
    flops = 6 * cells * cols_here * slots
    return vmem_call(gather_kernel, shape, flops, 4 * (levels * slots + 2 * slots + cells * cols_here))(state2d, rows, cols)


def with_halo(block, sides, width):
    for axis, dim in sides:
        count = lax.axis_size(axis)
        forward = [(i, i + 1) for i in range(count - 1)]
        forward.append((count - 1, 0))
        backward = [(target, source) for source, target in forward]
        low = lax.slice_in_dim(block, block.shape[dim] - width, None, axis=dim)
        high = lax.slice_in_dim(block, 0, width, axis=dim)
        if dim == block.ndim - 1:
            flat = block.shape[:-2] + (-1,)
            low = lax.ppermute(low.reshape(flat), axis, forward).reshape(low.shape)
            high = lax.ppermute(high.reshape(flat), axis, backward).reshape(high.shape)
        else:
            low = lax.ppermute(low, axis, forward)
            high = lax.ppermute(high, axis, backward)
        block = jnp.concatenate([low, block, high], axis=dim)
    return block


def one_pass(field, east_face, north_face, offset):
    high, wide = field.shape[1], field.shape[2]
    rows = slice(offset + 1, offset + high - 1)
    cols = slice(offset + 1, offset + wide - 1)
    centre = field[:, 1:-1, 1:-1]
    east_here = east_face[rows, cols]
    east_west = east_face[rows, offset : offset + wide - 2]
    north_here = north_face[rows, cols]
    north_south = north_face[offset : offset + high - 2, cols]
    return (
        centre
        + east_here * (field[:, 1:-1, 2:] - centre)
        - east_west * (centre - field[:, 1:-1, :-2])
        + north_here * (field[:, 2:, 1:-1] - centre)
        - north_south * (centre - field[:, :-2, 1:-1])
    )


def body(state, coef_lon, coef_lat, land_sea, send_cols, send_count, obs_value, obs_weight):
    levels, rows_here, cols_here = state.shape
    lon_count = lax.axis_size("lon")
    lat_count = lax.axis_size("lat")
    slots = send_cols.shape[1]
    capacity = slots // lon_count
    targets = send_cols[0]
    slot_index = jnp.arange(slots, dtype=jnp.int32)
    limits = jnp.broadcast_to(send_count[0][:, None], (lon_count, capacity)).reshape(slots)
    usable = jnp.where(slot_index % capacity < limits, 1.0, 0.0).astype(jnp.float32)
    chunked = (levels, lon_count, capacity)
    held = jnp.concatenate(
        [obs_value[:, 0, :].reshape(chunked), obs_weight[:, 0, :].reshape(chunked)], axis=2
    ).reshape(levels, 2 * slots)
    at_owner = lax.all_to_all(held, "lon", split_axis=1, concat_axis=1, tiled=True)
    at_owner = at_owner.reshape(levels, lon_count, 2 * capacity)
    values = at_owner[:, :, :capacity].reshape(levels, slots)
    weights = at_owner[:, :, capacity:].reshape(levels, slots)
    target_rows = (targets // cols_here)[None, :]
    target_cols = (targets % cols_here)[None, :]
    at_column = onehot_gather(state.reshape(levels * rows_here, cols_here), target_rows, target_cols, levels)
    sea = land_sea.astype(jnp.float32)
    gradient = onehot_scatter(values, weights, at_column, usable[None, :], target_rows, target_cols, sea)
    rim_width = PASSES
    stacked = jnp.concatenate([gradient, sea[None], coef_lon[None], coef_lat[None]], axis=0)
    padded = with_halo(stacked, (("lon", 2), ("lat", 1)), rim_width)
    field = padded[:levels]
    padded = padded[levels:]
    lat_index = lax.axis_index("lat")
    row_place = jnp.arange(rows_here + 2 * rim_width, dtype=jnp.int32)
    outside = (row_place < rim_width) & (lat_index == 0) | (row_place >= rows_here + rim_width) & (
        lat_index == lat_count - 1
    )
    inside = jnp.where(outside, 0.0, 1.0).astype(jnp.float32)[:, None]
    sea_rim = padded[0] * inside
    east_face = padded[1][:, :-1] * sea_rim[:, :-1] * sea_rim[:, 1:]
    north_face = padded[2][:-1, :] * sea_rim[:-1, :] * sea_rim[1:, :]
    for step_number in range(PASSES):
        field = one_pass(field, east_face, north_face, step_number)
    gradient = field
    return gradient


def solution(mesh):
    placed = (
        P(None, "lat", "lon"),
        P("lat", "lon"),
        P("lat", "lon"),
        P("lat", "lon"),
        P("lat", "lon"),
        P("lat", "lon"),
        P(None, "lat", "lon"),
        P(None, "lat", "lon"),
    )
    return jax.shard_map(
        body, mesh=mesh, in_specs=placed, out_specs=P(None, "lat", "lon"), check_vma=False
    )
```

```python
import jax
import jax.numpy as jnp
from jax import lax
from jax.experimental import pallas as pl
from jax.experimental.pallas import tpu as pltpu
from jax.sharding import PartitionSpec as P

PASSES = 8
CHUNK = 512
SCATTER_CHUNK = 1024


def three_parts(x):
    high = x.astype(jnp.bfloat16)
    rest = x - high.astype(jnp.float32)
    middle = rest.astype(jnp.bfloat16)
    low = (rest - middle.astype(jnp.float32)).astype(jnp.bfloat16)
    return high, middle, low


def scatter_kernel(values_ref, weights_ref, seen_ref, usable_ref, rows_ref, cols_ref, sea_ref, out_ref, acc_ref):
    levels, slots = values_ref.shape
    _, rows_here, cols_here = out_ref.shape
    cells = levels * rows_here
    acc_ref[...] = jnp.zeros_like(acc_ref)

    def step(k, carry):
        start = pl.multiple_of(k * SCATTER_CHUNK, SCATTER_CHUNK)
        here = pl.ds(start, SCATTER_CHUNK)
        w = weights_ref[:, here] * (values_ref[:, here] - seen_ref[:, here]) * usable_ref[:, here]
        row_hit = lax.broadcasted_iota(jnp.int32, (rows_here, SCATTER_CHUNK), 0) == rows_ref[:, here]
        col_hit = lax.broadcasted_iota(jnp.int32, (cols_here, SCATTER_CHUNK), 0) == cols_ref[:, here]
        col_hit = col_hit.astype(jnp.float32).astype(jnp.bfloat16)
        spread = [
            jnp.where(row_hit[None], part.astype(jnp.float32)[:, None, :], 0.0)
            .reshape(cells, SCATTER_CHUNK)
            .astype(jnp.bfloat16)
            for part in three_parts(w)
        ]
        acc_ref[...] += lax.dot_general(
            jnp.concatenate(spread, axis=1),
            jnp.concatenate([col_hit] * 3, axis=1),
            (((1,), (1,)), ((), ())),
            preferred_element_type=jnp.float32,
        )
        return carry

    lax.fori_loop(0, slots // SCATTER_CHUNK, step, 0)
    out_ref[...] = acc_ref[...].reshape(levels, rows_here, cols_here) * sea_ref[...][None]


def gather_kernel(state_ref, rows_ref, cols_ref, out_ref):
    levels, slots = out_ref.shape
    cells, cols_here = state_ref.shape
    rows_here = cells // levels
    parts = three_parts(state_ref[...])

    def step(k, carry):
        start = pl.multiple_of(k * CHUNK, CHUNK)
        col_hit = lax.broadcasted_iota(jnp.int32, (cols_here, CHUNK), 0) == cols_ref[:, pl.ds(start, CHUNK)]
        col_hit = col_hit.astype(jnp.float32).astype(jnp.bfloat16)
        picked = None
        for part in parts:
            term = jnp.dot(part, col_hit, preferred_element_type=jnp.float32)
            picked = term if picked is None else picked + term
        row_hit = lax.broadcasted_iota(jnp.int32, (rows_here, CHUNK), 0) == rows_ref[:, pl.ds(start, CHUNK)]
        chosen = jnp.where(row_hit[None], picked.reshape(levels, rows_here, CHUNK), 0.0)
        out_ref[:, pl.ds(start, CHUNK)] = jnp.sum(chosen, axis=1)
        return carry

    lax.fori_loop(0, slots // CHUNK, step, 0)


def vmem_call(kernel, out_shape, flops, nbytes):
    return pl.pallas_call(
        kernel,
        out_shape=out_shape,
        in_specs=[pl.BlockSpec(memory_space=pltpu.VMEM)] * 3,
        out_specs=pl.BlockSpec(memory_space=pltpu.VMEM),
        cost_estimate=pl.CostEstimate(flops=flops, bytes_accessed=nbytes, transcendentals=0),
    )


def onehot_scatter(values, weights, seen, usable, rows, cols, sea):
    levels, slots = values.shape
    rows_here, cols_here = sea.shape
    shape = jax.ShapeDtypeStruct((levels, rows_here, cols_here), jnp.float32)
    flops = 6 * levels * rows_here * cols_here * slots
    return pl.pallas_call(
        scatter_kernel,
        out_shape=shape,
        in_specs=[pl.BlockSpec(memory_space=pltpu.VMEM)] * 7,
        out_specs=pl.BlockSpec(memory_space=pltpu.VMEM),
        scratch_shapes=[pltpu.VMEM((levels * rows_here, cols_here), jnp.float32)],
        cost_estimate=pl.CostEstimate(
            flops=flops, bytes_accessed=4 * (3 * levels * slots + 3 * slots + levels * rows_here * cols_here),
            transcendentals=0,
        ),
    )(values, weights, seen, usable, rows, cols, sea)


def onehot_gather(state2d, rows, cols, levels):
    cells, cols_here = state2d.shape
    slots = rows.shape[1]
    shape = jax.ShapeDtypeStruct((levels, slots), jnp.float32)
    flops = 6 * cells * cols_here * slots
    return vmem_call(gather_kernel, shape, flops, 4 * (levels * slots + 2 * slots + cells * cols_here))(state2d, rows, cols)


def full_halo(block, width):
    lon_count = lax.axis_size("lon")
    lat_count = lax.axis_size("lat")

    def shift(piece, lon_step, lat_step):
        flat = piece.shape[:-2] + (-1,)
        pairs = [
            (i * lat_count + j, ((i + lon_step) % lon_count) * lat_count + (j + lat_step) % lat_count)
            for i in range(lon_count)
            for j in range(lat_count)
        ]
        moved = lax.ppermute(piece.reshape(flat) if piece.shape[-1] == width else piece, ("lon", "lat"), pairs)
        return moved.reshape(piece.shape)

    low_rows = block[..., -width:, :]
    high_rows = block[..., :width, :]
    south = shift(low_rows, 0, 1)
    north = shift(high_rows, 0, -1)
    west = shift(block[..., -width:], 1, 0)
    east = shift(block[..., :width], -1, 0)
    south_west = shift(low_rows[..., -width:], 1, 1)
    south_east = shift(low_rows[..., :width], -1, 1)
    north_west = shift(high_rows[..., -width:], 1, -1)
    north_east = shift(high_rows[..., :width], -1, -1)
    return jnp.concatenate(
        [
            jnp.concatenate([south_west, south, south_east], axis=-1),
            jnp.concatenate([west, block, east], axis=-1),
            jnp.concatenate([north_west, north, north_east], axis=-1),
        ],
        axis=-2,
    )


def one_pass(field, east_face, north_face, offset):
    high, wide = field.shape[1], field.shape[2]
    rows = slice(offset + 1, offset + high - 1)
    cols = slice(offset + 1, offset + wide - 1)
    centre = field[:, 1:-1, 1:-1]
    east_here = east_face[rows, cols]
    east_west = east_face[rows, offset : offset + wide - 2]
    north_here = north_face[rows, cols]
    north_south = north_face[offset : offset + high - 2, cols]
    return (
        centre
        + east_here * (field[:, 1:-1, 2:] - centre)
        - east_west * (centre - field[:, 1:-1, :-2])
        + north_here * (field[:, 2:, 1:-1] - centre)
        - north_south * (centre - field[:, :-2, 1:-1])
    )


def body(state, coef_lon, coef_lat, land_sea, send_cols, send_count, obs_value, obs_weight):
    levels, rows_here, cols_here = state.shape
    lon_count = lax.axis_size("lon")
    lat_count = lax.axis_size("lat")
    slots = send_cols.shape[1]
    capacity = slots // lon_count
    targets = send_cols[0]
    slot_index = jnp.arange(slots, dtype=jnp.int32)
    limits = jnp.broadcast_to(send_count[0][:, None], (lon_count, capacity)).reshape(slots)
    usable = jnp.where(slot_index % capacity < limits, 1.0, 0.0).astype(jnp.float32)
    chunked = (levels, lon_count, capacity)
    held = jnp.concatenate(
        [obs_value[:, 0, :].reshape(chunked), obs_weight[:, 0, :].reshape(chunked)], axis=2
    ).reshape(levels, 2 * slots)
    at_owner = lax.all_to_all(held, "lon", split_axis=1, concat_axis=1, tiled=True)
    at_owner = at_owner.reshape(levels, lon_count, 2 * capacity)
    values = at_owner[:, :, :capacity].reshape(levels, slots)
    weights = at_owner[:, :, capacity:].reshape(levels, slots)
    target_rows = (targets // cols_here)[None, :]
    target_cols = (targets % cols_here)[None, :]
    at_column = onehot_gather(state.reshape(levels * rows_here, cols_here), target_rows, target_cols, levels)
    sea = land_sea.astype(jnp.float32)
    gradient = onehot_scatter(values, weights, at_column, usable[None, :], target_rows, target_cols, sea)
    rim_width = PASSES
    stacked = jnp.concatenate([gradient, sea[None], coef_lon[None], coef_lat[None]], axis=0)
    padded = full_halo(stacked, rim_width)
    field = padded[:levels]
    padded = padded[levels:]
    lat_index = lax.axis_index("lat")
    row_place = jnp.arange(rows_here + 2 * rim_width, dtype=jnp.int32)
    outside = (row_place < rim_width) & (lat_index == 0) | (row_place >= rows_here + rim_width) & (
        lat_index == lat_count - 1
    )
    inside = jnp.where(outside, 0.0, 1.0).astype(jnp.float32)[:, None]
    sea_rim = padded[0] * inside
    east_face = padded[1][:, :-1] * sea_rim[:, :-1] * sea_rim[:, 1:]
    north_face = padded[2][:-1, :] * sea_rim[:-1, :] * sea_rim[1:, :]
    for step_number in range(PASSES):
        field = one_pass(field, east_face, north_face, step_number)
    gradient = field
    return gradient


def solution(mesh):
    placed = (
        P(None, "lat", "lon"),
        P("lat", "lon"),
        P("lat", "lon"),
        P("lat", "lon"),
        P("lat", "lon"),
        P("lat", "lon"),
        P(None, "lat", "lon"),
        P(None, "lat", "lon"),
    )
    return jax.shard_map(
        body, mesh=mesh, in_specs=placed, out_specs=P(None, "lat", "lon"), check_vma=False
    )
```

```python
import jax
import jax.numpy as jnp
from jax import lax
from jax.experimental import pallas as pl
from jax.experimental.pallas import tpu as pltpu
from jax.sharding import PartitionSpec as P

PASSES = 8
CHUNK = 512
SCATTER_CHUNK = 1024


def three_parts(x):
    high = x.astype(jnp.bfloat16)
    rest = x - high.astype(jnp.float32)
    middle = rest.astype(jnp.bfloat16)
    low = (rest - middle.astype(jnp.float32)).astype(jnp.bfloat16)
    return high, middle, low


def scatter_kernel(held_ref, seen_ref, usable_ref, rows_ref, cols_ref, sea_ref, out_ref, acc_ref):
    levels, slots = seen_ref.shape
    peers, _, pair = held_ref.shape
    capacity = pair // 2
    per_chunk = SCATTER_CHUNK // capacity
    _, rows_here, cols_here = out_ref.shape
    cells = levels * rows_here
    acc_ref[...] = jnp.zeros_like(acc_ref)

    def step(k, carry):
        start = pl.multiple_of(k * SCATTER_CHUNK, SCATTER_CHUNK)
        here = pl.ds(start, SCATTER_CHUNK)
        held = [held_ref[k * per_chunk + i] for i in range(per_chunk)]
        values = jnp.concatenate([h[:, :capacity] for h in held], axis=1)
        weights = jnp.concatenate([h[:, capacity:] for h in held], axis=1)
        w = weights * (values - seen_ref[:, here]) * usable_ref[:, here]
        row_hit = lax.broadcasted_iota(jnp.int32, (rows_here, SCATTER_CHUNK), 0) == rows_ref[:, here]
        col_hit = lax.broadcasted_iota(jnp.int32, (cols_here, SCATTER_CHUNK), 0) == cols_ref[:, here]
        col_hit = col_hit.astype(jnp.float32).astype(jnp.bfloat16)
        spread = [
            jnp.where(row_hit[None], part.astype(jnp.float32)[:, None, :], 0.0)
            .reshape(cells, SCATTER_CHUNK)
            .astype(jnp.bfloat16)
            for part in three_parts(w)
        ]
        acc_ref[...] += lax.dot_general(
            jnp.concatenate(spread, axis=1),
            jnp.concatenate([col_hit] * 3, axis=1),
            (((1,), (1,)), ((), ())),
            preferred_element_type=jnp.float32,
        )
        return carry

    lax.fori_loop(0, slots // SCATTER_CHUNK, step, 0)
    out_ref[...] = acc_ref[...].reshape(levels, rows_here, cols_here) * sea_ref[...][None]


def gather_kernel(state_ref, rows_ref, cols_ref, out_ref):
    levels, slots = out_ref.shape
    cells, cols_here = state_ref.shape
    rows_here = cells // levels
    parts = three_parts(state_ref[...])

    def step(k, carry):
        start = pl.multiple_of(k * CHUNK, CHUNK)
        col_hit = lax.broadcasted_iota(jnp.int32, (cols_here, CHUNK), 0) == cols_ref[:, pl.ds(start, CHUNK)]
        col_hit = col_hit.astype(jnp.float32).astype(jnp.bfloat16)
        picked = None
        for part in parts:
            term = jnp.dot(part, col_hit, preferred_element_type=jnp.float32)
            picked = term if picked is None else picked + term
        row_hit = lax.broadcasted_iota(jnp.int32, (rows_here, CHUNK), 0) == rows_ref[:, pl.ds(start, CHUNK)]
        chosen = jnp.where(row_hit[None], picked.reshape(levels, rows_here, CHUNK), 0.0)
        out_ref[:, pl.ds(start, CHUNK)] = jnp.sum(chosen, axis=1)
        return carry

    lax.fori_loop(0, slots // CHUNK, step, 0)


def vmem_call(kernel, out_shape, flops, nbytes):
    return pl.pallas_call(
        kernel,
        out_shape=out_shape,
        in_specs=[pl.BlockSpec(memory_space=pltpu.VMEM)] * 3,
        out_specs=pl.BlockSpec(memory_space=pltpu.VMEM),
        cost_estimate=pl.CostEstimate(flops=flops, bytes_accessed=nbytes, transcendentals=0),
    )


def onehot_scatter(held, seen, usable, rows, cols, sea):
    levels, slots = seen.shape
    rows_here, cols_here = sea.shape
    shape = jax.ShapeDtypeStruct((levels, rows_here, cols_here), jnp.float32)
    flops = 6 * levels * rows_here * cols_here * slots
    return pl.pallas_call(
        scatter_kernel,
        out_shape=shape,
        in_specs=[pl.BlockSpec(memory_space=pltpu.VMEM)] * 6,
        out_specs=pl.BlockSpec(memory_space=pltpu.VMEM),
        scratch_shapes=[pltpu.VMEM((levels * rows_here, cols_here), jnp.float32)],
        cost_estimate=pl.CostEstimate(
            flops=flops, bytes_accessed=4 * (3 * levels * slots + 3 * slots + levels * rows_here * cols_here),
            transcendentals=0,
        ),
    )(held, seen, usable, rows, cols, sea)


def onehot_gather(state2d, rows, cols, levels):
    cells, cols_here = state2d.shape
    slots = rows.shape[1]
    shape = jax.ShapeDtypeStruct((levels, slots), jnp.float32)
    flops = 6 * cells * cols_here * slots
    return vmem_call(gather_kernel, shape, flops, 4 * (levels * slots + 2 * slots + cells * cols_here))(state2d, rows, cols)


def with_halo(block, sides, width):
    for axis, dim in sides:
        count = lax.axis_size(axis)
        forward = [(i, i + 1) for i in range(count - 1)]
        forward.append((count - 1, 0))
        backward = [(target, source) for source, target in forward]
        low = lax.slice_in_dim(block, block.shape[dim] - width, None, axis=dim)
        high = lax.slice_in_dim(block, 0, width, axis=dim)
        if dim == block.ndim - 1:
            flat = block.shape[:-2] + (-1,)
            low = lax.ppermute(low.reshape(flat), axis, forward).reshape(low.shape)
            high = lax.ppermute(high.reshape(flat), axis, backward).reshape(high.shape)
        else:
            low = lax.ppermute(low, axis, forward)
            high = lax.ppermute(high, axis, backward)
        block = jnp.concatenate([low, block, high], axis=dim)
    return block


def one_pass(field, east_face, north_face, offset):
    high, wide = field.shape[1], field.shape[2]
    rows = slice(offset + 1, offset + high - 1)
    cols = slice(offset + 1, offset + wide - 1)
    centre = field[:, 1:-1, 1:-1]
    east_here = east_face[rows, cols]
    east_west = east_face[rows, offset : offset + wide - 2]
    north_here = north_face[rows, cols]
    north_south = north_face[offset : offset + high - 2, cols]
    return (
        centre
        + east_here * (field[:, 1:-1, 2:] - centre)
        - east_west * (centre - field[:, 1:-1, :-2])
        + north_here * (field[:, 2:, 1:-1] - centre)
        - north_south * (centre - field[:, :-2, 1:-1])
    )


def body(state, coef_lon, coef_lat, land_sea, send_cols, send_count, obs_value, obs_weight):
    levels, rows_here, cols_here = state.shape
    lon_count = lax.axis_size("lon")
    lat_count = lax.axis_size("lat")
    slots = send_cols.shape[1]
    capacity = slots // lon_count
    targets = send_cols[0]
    slot_index = jnp.arange(slots, dtype=jnp.int32)
    limits = jnp.broadcast_to(send_count[0][:, None], (lon_count, capacity)).reshape(slots)
    usable = jnp.where(slot_index % capacity < limits, 1.0, 0.0).astype(jnp.float32)
    chunked = (levels, lon_count, capacity)
    held = jnp.concatenate([obs_value.reshape(chunked), obs_weight.reshape(chunked)], axis=2)
    held = jnp.transpose(held, (1, 0, 2))
    at_owner = lax.all_to_all(held, "lon", split_axis=0, concat_axis=0, tiled=True)
    target_rows = (targets // cols_here)[None, :]
    target_cols = (targets % cols_here)[None, :]
    at_column = onehot_gather(state.reshape(levels * rows_here, cols_here), target_rows, target_cols, levels)
    sea = land_sea.astype(jnp.float32)
    gradient = onehot_scatter(at_owner, at_column, usable[None, :], target_rows, target_cols, sea)
    rim_width = PASSES
    stacked = jnp.concatenate([gradient, sea[None], coef_lon[None], coef_lat[None]], axis=0)
    padded = with_halo(stacked, (("lon", 2), ("lat", 1)), rim_width)
    field = padded[:levels]
    padded = padded[levels:]
    lat_index = lax.axis_index("lat")
    row_place = jnp.arange(rows_here + 2 * rim_width, dtype=jnp.int32)
    outside = (row_place < rim_width) & (lat_index == 0) | (row_place >= rows_here + rim_width) & (
        lat_index == lat_count - 1
    )
    inside = jnp.where(outside, 0.0, 1.0).astype(jnp.float32)[:, None]
    sea_rim = padded[0] * inside
    east_face = padded[1][:, :-1] * sea_rim[:, :-1] * sea_rim[:, 1:]
    north_face = padded[2][:-1, :] * sea_rim[:-1, :] * sea_rim[1:, :]
    for step_number in range(PASSES):
        field = one_pass(field, east_face, north_face, step_number)
    gradient = field
    return gradient


def solution(mesh):
    placed = (
        P(None, "lat", "lon"),
        P("lat", "lon"),
        P("lat", "lon"),
        P("lat", "lon"),
        P("lat", "lon"),
        P("lat", "lon"),
        P(None, "lat", "lon"),
        P(None, "lat", "lon"),
    )
    return jax.shard_map(
        body, mesh=mesh, in_specs=placed, out_specs=P(None, "lat", "lon"), check_vma=False
    )
```

```python
import jax
import jax.numpy as jnp
from jax import lax
from jax.experimental import pallas as pl
from jax.experimental.pallas import tpu as pltpu
from jax.sharding import PartitionSpec as P

PASSES = 8
CHUNK = 512
SCATTER_CHUNK = 1024


def three_parts(x):
    high = x.astype(jnp.bfloat16)
    rest = x - high.astype(jnp.float32)
    middle = rest.astype(jnp.bfloat16)
    low = (rest - middle.astype(jnp.float32)).astype(jnp.bfloat16)
    return high, middle, low


def scatter_kernel(held_ref, seen_ref, usable_ref, rows_ref, cols_ref, sea_ref, out_ref, acc_ref):
    levels, slots = seen_ref.shape
    peers, _, pair = held_ref.shape
    capacity = pair // 2
    per_chunk = SCATTER_CHUNK // capacity
    _, rows_here, cols_here = out_ref.shape
    cells = levels * rows_here
    acc_ref[...] = jnp.zeros_like(acc_ref)

    def step(k, carry):
        start = pl.multiple_of(k * SCATTER_CHUNK, SCATTER_CHUNK)
        here = pl.ds(start, SCATTER_CHUNK)
        held = [held_ref[k * per_chunk + i] for i in range(per_chunk)]
        values = jnp.concatenate([h[:, :capacity] for h in held], axis=1)
        weights = jnp.concatenate([h[:, capacity:] for h in held], axis=1)
        w = weights * (values - seen_ref[:, here]) * usable_ref[:, here]
        row_hit = lax.broadcasted_iota(jnp.int32, (rows_here, SCATTER_CHUNK), 0) == rows_ref[:, here]
        col_hit = lax.broadcasted_iota(jnp.int32, (cols_here, SCATTER_CHUNK), 0) == cols_ref[:, here]
        col_hit = col_hit.astype(jnp.float32).astype(jnp.bfloat16)
        spread = [
            jnp.where(row_hit[None], part.astype(jnp.float32)[:, None, :], 0.0)
            .reshape(cells, SCATTER_CHUNK)
            .astype(jnp.bfloat16)
            for part in three_parts(w)
        ]
        acc_ref[...] += lax.dot_general(
            jnp.concatenate(spread, axis=1),
            jnp.concatenate([col_hit] * 3, axis=1),
            (((1,), (1,)), ((), ())),
            preferred_element_type=jnp.float32,
        )
        return carry

    lax.fori_loop(0, slots // SCATTER_CHUNK, step, 0)
    out_ref[...] = acc_ref[...].reshape(levels, rows_here, cols_here) * sea_ref[...][None]


def gather_kernel(state_ref, rows_ref, cols_ref, out_ref):
    levels, slots = out_ref.shape
    cells, cols_here = state_ref.shape
    rows_here = cells // levels
    parts = three_parts(state_ref[...])

    def step(k, carry):
        start = pl.multiple_of(k * CHUNK, CHUNK)
        col_hit = lax.broadcasted_iota(jnp.int32, (cols_here, CHUNK), 0) == cols_ref[:, pl.ds(start, CHUNK)]
        col_hit = col_hit.astype(jnp.float32).astype(jnp.bfloat16)
        picked = None
        for part in parts:
            term = jnp.dot(part, col_hit, preferred_element_type=jnp.float32)
            picked = term if picked is None else picked + term
        row_hit = lax.broadcasted_iota(jnp.int32, (rows_here, CHUNK), 0) == rows_ref[:, pl.ds(start, CHUNK)]
        chosen = jnp.where(row_hit[None], picked.reshape(levels, rows_here, CHUNK), 0.0)
        out_ref[:, pl.ds(start, CHUNK)] = jnp.sum(chosen, axis=1)
        return carry

    lax.fori_loop(0, slots // CHUNK, step, 0)


def vmem_call(kernel, out_shape, flops, nbytes):
    return pl.pallas_call(
        kernel,
        out_shape=out_shape,
        in_specs=[pl.BlockSpec(memory_space=pltpu.VMEM)] * 3,
        out_specs=pl.BlockSpec(memory_space=pltpu.VMEM),
        cost_estimate=pl.CostEstimate(flops=flops, bytes_accessed=nbytes, transcendentals=0),
    )


def onehot_scatter(held, seen, usable, rows, cols, sea):
    levels, slots = seen.shape
    rows_here, cols_here = sea.shape
    shape = jax.ShapeDtypeStruct((levels, rows_here, cols_here), jnp.float32)
    flops = 6 * levels * rows_here * cols_here * slots
    return pl.pallas_call(
        scatter_kernel,
        out_shape=shape,
        in_specs=[pl.BlockSpec(memory_space=pltpu.VMEM)] * 6,
        out_specs=pl.BlockSpec(memory_space=pltpu.VMEM),
        scratch_shapes=[pltpu.VMEM((levels * rows_here, cols_here), jnp.float32)],
        cost_estimate=pl.CostEstimate(
            flops=flops, bytes_accessed=4 * (3 * levels * slots + 3 * slots + levels * rows_here * cols_here),
            transcendentals=0,
        ),
    )(held, seen, usable, rows, cols, sea)


def onehot_gather(state2d, rows, cols, levels):
    cells, cols_here = state2d.shape
    slots = rows.shape[1]
    shape = jax.ShapeDtypeStruct((levels, slots), jnp.float32)
    flops = 6 * cells * cols_here * slots
    return vmem_call(gather_kernel, shape, flops, 4 * (levels * slots + 2 * slots + cells * cols_here))(state2d, rows, cols)


def pack_kernel(values_ref, weights_ref, out_ref):
    peers, _, pair = out_ref.shape
    capacity = pair // 2
    for peer in range(peers):
        here = slice(peer * capacity, (peer + 1) * capacity)
        out_ref[peer, :, :capacity] = values_ref[:, 0, here]
        out_ref[peer, :, capacity:] = weights_ref[:, 0, here]


def pack_for_owners(values, weights, peers):
    levels, _, slots = values.shape
    capacity = slots // peers
    return pl.pallas_call(
        pack_kernel,
        out_shape=jax.ShapeDtypeStruct((peers, levels, 2 * capacity), jnp.float32),
        in_specs=[pl.BlockSpec(memory_space=pltpu.VMEM)] * 2,
        out_specs=pl.BlockSpec(memory_space=pltpu.VMEM),
        cost_estimate=pl.CostEstimate(flops=0, bytes_accessed=16 * levels * slots, transcendentals=0),
    )(values, weights)


def with_halo(block, sides, width):
    for axis, dim in sides:
        count = lax.axis_size(axis)
        forward = [(i, i + 1) for i in range(count - 1)]
        forward.append((count - 1, 0))
        backward = [(target, source) for source, target in forward]
        low = lax.slice_in_dim(block, block.shape[dim] - width, None, axis=dim)
        high = lax.slice_in_dim(block, 0, width, axis=dim)
        if dim == block.ndim - 1:
            flat = block.shape[:-2] + (-1,)
            low = lax.ppermute(low.reshape(flat), axis, forward).reshape(low.shape)
            high = lax.ppermute(high.reshape(flat), axis, backward).reshape(high.shape)
        else:
            low = lax.ppermute(low, axis, forward)
            high = lax.ppermute(high, axis, backward)
        block = jnp.concatenate([low, block, high], axis=dim)
    return block


def one_pass(field, east_face, north_face, offset):
    high, wide = field.shape[1], field.shape[2]
    rows = slice(offset + 1, offset + high - 1)
    cols = slice(offset + 1, offset + wide - 1)
    centre = field[:, 1:-1, 1:-1]
    east_here = east_face[rows, cols]
    east_west = east_face[rows, offset : offset + wide - 2]
    north_here = north_face[rows, cols]
    north_south = north_face[offset : offset + high - 2, cols]
    return (
        centre
        + east_here * (field[:, 1:-1, 2:] - centre)
        - east_west * (centre - field[:, 1:-1, :-2])
        + north_here * (field[:, 2:, 1:-1] - centre)
        - north_south * (centre - field[:, :-2, 1:-1])
    )


def body(state, coef_lon, coef_lat, land_sea, send_cols, send_count, obs_value, obs_weight):
    levels, rows_here, cols_here = state.shape
    lon_count = lax.axis_size("lon")
    lat_count = lax.axis_size("lat")
    slots = send_cols.shape[1]
    capacity = slots // lon_count
    targets = send_cols[0]
    slot_index = jnp.arange(slots, dtype=jnp.int32)
    limits = jnp.broadcast_to(send_count[0][:, None], (lon_count, capacity)).reshape(slots)
    usable = jnp.where(slot_index % capacity < limits, 1.0, 0.0).astype(jnp.float32)
    held = pack_for_owners(obs_value, obs_weight, lon_count)
    at_owner = lax.all_to_all(held, "lon", split_axis=0, concat_axis=0, tiled=True)
    target_rows = (targets // cols_here)[None, :]
    target_cols = (targets % cols_here)[None, :]
    at_column = onehot_gather(state.reshape(levels * rows_here, cols_here), target_rows, target_cols, levels)
    sea = land_sea.astype(jnp.float32)
    gradient = onehot_scatter(at_owner, at_column, usable[None, :], target_rows, target_cols, sea)
    rim_width = PASSES
    stacked = jnp.concatenate([gradient, sea[None], coef_lon[None], coef_lat[None]], axis=0)
    padded = with_halo(stacked, (("lon", 2), ("lat", 1)), rim_width)
    field = padded[:levels]
    padded = padded[levels:]
    lat_index = lax.axis_index("lat")
    row_place = jnp.arange(rows_here + 2 * rim_width, dtype=jnp.int32)
    outside = (row_place < rim_width) & (lat_index == 0) | (row_place >= rows_here + rim_width) & (
        lat_index == lat_count - 1
    )
    inside = jnp.where(outside, 0.0, 1.0).astype(jnp.float32)[:, None]
    sea_rim = padded[0] * inside
    east_face = padded[1][:, :-1] * sea_rim[:, :-1] * sea_rim[:, 1:]
    north_face = padded[2][:-1, :] * sea_rim[:-1, :] * sea_rim[1:, :]
    for step_number in range(PASSES):
        field = one_pass(field, east_face, north_face, step_number)
    gradient = field
    return gradient


def solution(mesh):
    placed = (
        P(None, "lat", "lon"),
        P("lat", "lon"),
        P("lat", "lon"),
        P("lat", "lon"),
        P("lat", "lon"),
        P("lat", "lon"),
        P(None, "lat", "lon"),
        P(None, "lat", "lon"),
    )
    return jax.shard_map(
        body, mesh=mesh, in_specs=placed, out_specs=P(None, "lat", "lon"), check_vma=False
    )
```

```python
import jax
import jax.numpy as jnp
from jax import lax
from jax.experimental import pallas as pl
from jax.experimental.pallas import tpu as pltpu
from jax.sharding import PartitionSpec as P

PASSES = 8
CHUNK = 512
SCATTER_CHUNK = 1024


def three_parts(x):
    high = x.astype(jnp.bfloat16)
    rest = x - high.astype(jnp.float32)
    middle = rest.astype(jnp.bfloat16)
    low = (rest - middle.astype(jnp.float32)).astype(jnp.bfloat16)
    return high, middle, low


def scatter_kernel(
    held_ref, seen_ref, usable_ref, rows_ref, cols_ref, sea_ref, coef_lon_ref, coef_lat_ref, out_ref, acc_ref
):
    levels, slots = seen_ref.shape
    peers, _, pair = held_ref.shape
    capacity = pair // 2
    per_chunk = SCATTER_CHUNK // capacity
    _, rows_here, cols_here = out_ref.shape
    cells = levels * rows_here
    acc_ref[...] = jnp.zeros_like(acc_ref)

    def step(k, carry):
        start = pl.multiple_of(k * SCATTER_CHUNK, SCATTER_CHUNK)
        here = pl.ds(start, SCATTER_CHUNK)
        held = [held_ref[k * per_chunk + i] for i in range(per_chunk)]
        values = jnp.concatenate([h[:, :capacity] for h in held], axis=1)
        weights = jnp.concatenate([h[:, capacity:] for h in held], axis=1)
        w = weights * (values - seen_ref[:, here]) * usable_ref[:, here]
        row_hit = lax.broadcasted_iota(jnp.int32, (rows_here, SCATTER_CHUNK), 0) == rows_ref[:, here]
        col_hit = lax.broadcasted_iota(jnp.int32, (cols_here, SCATTER_CHUNK), 0) == cols_ref[:, here]
        col_hit = col_hit.astype(jnp.float32).astype(jnp.bfloat16)
        spread = [
            jnp.where(row_hit[None], part.astype(jnp.float32)[:, None, :], 0.0)
            .reshape(cells, SCATTER_CHUNK)
            .astype(jnp.bfloat16)
            for part in three_parts(w)
        ]
        acc_ref[...] += lax.dot_general(
            jnp.concatenate(spread, axis=1),
            jnp.concatenate([col_hit] * 3, axis=1),
            (((1,), (1,)), ((), ())),
            preferred_element_type=jnp.float32,
        )
        return carry

    lax.fori_loop(0, slots // SCATTER_CHUNK, step, 0)
    out_ref[:levels] = acc_ref[...].reshape(levels, rows_here, cols_here) * sea_ref[...][None]
    out_ref[levels] = sea_ref[...]
    out_ref[levels + 1] = coef_lon_ref[...]
    out_ref[levels + 2] = coef_lat_ref[...]


def gather_kernel(state_ref, rows_ref, cols_ref, out_ref):
    levels, slots = out_ref.shape
    cells, cols_here = state_ref.shape
    rows_here = cells // levels
    parts = three_parts(state_ref[...])

    def step(k, carry):
        start = pl.multiple_of(k * CHUNK, CHUNK)
        col_hit = lax.broadcasted_iota(jnp.int32, (cols_here, CHUNK), 0) == cols_ref[:, pl.ds(start, CHUNK)]
        col_hit = col_hit.astype(jnp.float32).astype(jnp.bfloat16)
        picked = None
        for part in parts:
            term = jnp.dot(part, col_hit, preferred_element_type=jnp.float32)
            picked = term if picked is None else picked + term
        row_hit = lax.broadcasted_iota(jnp.int32, (rows_here, CHUNK), 0) == rows_ref[:, pl.ds(start, CHUNK)]
        chosen = jnp.where(row_hit[None], picked.reshape(levels, rows_here, CHUNK), 0.0)
        out_ref[:, pl.ds(start, CHUNK)] = jnp.sum(chosen, axis=1)
        return carry

    lax.fori_loop(0, slots // CHUNK, step, 0)


def vmem_call(kernel, out_shape, flops, nbytes):
    return pl.pallas_call(
        kernel,
        out_shape=out_shape,
        in_specs=[pl.BlockSpec(memory_space=pltpu.VMEM)] * 3,
        out_specs=pl.BlockSpec(memory_space=pltpu.VMEM),
        cost_estimate=pl.CostEstimate(flops=flops, bytes_accessed=nbytes, transcendentals=0),
    )


def onehot_scatter(held, seen, usable, rows, cols, sea, coef_lon, coef_lat):
    levels, slots = seen.shape
    rows_here, cols_here = sea.shape
    shape = jax.ShapeDtypeStruct((levels + 3, rows_here, cols_here), jnp.float32)
    flops = 6 * levels * rows_here * cols_here * slots
    return pl.pallas_call(
        scatter_kernel,
        out_shape=shape,
        in_specs=[pl.BlockSpec(memory_space=pltpu.VMEM)] * 8,
        out_specs=pl.BlockSpec(memory_space=pltpu.VMEM),
        scratch_shapes=[pltpu.VMEM((levels * rows_here, cols_here), jnp.float32)],
        cost_estimate=pl.CostEstimate(
            flops=flops, bytes_accessed=4 * (3 * levels * slots + 3 * slots + levels * rows_here * cols_here),
            transcendentals=0,
        ),
    )(held, seen, usable, rows, cols, sea, coef_lon, coef_lat)


def onehot_gather(state2d, rows, cols, levels):
    cells, cols_here = state2d.shape
    slots = rows.shape[1]
    shape = jax.ShapeDtypeStruct((levels, slots), jnp.float32)
    flops = 6 * cells * cols_here * slots
    return vmem_call(gather_kernel, shape, flops, 4 * (levels * slots + 2 * slots + cells * cols_here))(state2d, rows, cols)


def with_halo(block, sides, width):
    for axis, dim in sides:
        count = lax.axis_size(axis)
        forward = [(i, i + 1) for i in range(count - 1)]
        forward.append((count - 1, 0))
        backward = [(target, source) for source, target in forward]
        low = lax.slice_in_dim(block, block.shape[dim] - width, None, axis=dim)
        high = lax.slice_in_dim(block, 0, width, axis=dim)
        if dim == block.ndim - 1:
            flat = block.shape[:-2] + (-1,)
            low = lax.ppermute(low.reshape(flat), axis, forward).reshape(low.shape)
            high = lax.ppermute(high.reshape(flat), axis, backward).reshape(high.shape)
        else:
            low = lax.ppermute(low, axis, forward)
            high = lax.ppermute(high, axis, backward)
        block = jnp.concatenate([low, block, high], axis=dim)
    return block


def one_pass(field, east_face, north_face, offset):
    high, wide = field.shape[1], field.shape[2]
    rows = slice(offset + 1, offset + high - 1)
    cols = slice(offset + 1, offset + wide - 1)
    centre = field[:, 1:-1, 1:-1]
    east_here = east_face[rows, cols]
    east_west = east_face[rows, offset : offset + wide - 2]
    north_here = north_face[rows, cols]
    north_south = north_face[offset : offset + high - 2, cols]
    return (
        centre
        + east_here * (field[:, 1:-1, 2:] - centre)
        - east_west * (centre - field[:, 1:-1, :-2])
        + north_here * (field[:, 2:, 1:-1] - centre)
        - north_south * (centre - field[:, :-2, 1:-1])
    )


def body(state, coef_lon, coef_lat, land_sea, send_cols, send_count, obs_value, obs_weight):
    levels, rows_here, cols_here = state.shape
    lon_count = lax.axis_size("lon")
    lat_count = lax.axis_size("lat")
    slots = send_cols.shape[1]
    capacity = slots // lon_count
    targets = send_cols[0]
    slot_index = jnp.arange(slots, dtype=jnp.int32)
    limits = jnp.broadcast_to(send_count[0][:, None], (lon_count, capacity)).reshape(slots)
    usable = jnp.where(slot_index % capacity < limits, 1.0, 0.0).astype(jnp.float32)
    chunked = (levels, lon_count, capacity)
    held = jnp.concatenate([obs_value.reshape(chunked), obs_weight.reshape(chunked)], axis=2)
    held = jnp.transpose(held, (1, 0, 2))
    at_owner = lax.all_to_all(held, "lon", split_axis=0, concat_axis=0, tiled=True)
    target_rows = (targets // cols_here)[None, :]
    target_cols = (targets % cols_here)[None, :]
    at_column = onehot_gather(state.reshape(levels * rows_here, cols_here), target_rows, target_cols, levels)
    sea = land_sea.astype(jnp.float32)
    stacked = onehot_scatter(at_owner, at_column, usable[None, :], target_rows, target_cols, sea, coef_lon, coef_lat)
    rim_width = PASSES
    padded = with_halo(stacked, (("lon", 2), ("lat", 1)), rim_width)
    field = padded[:levels]
    padded = padded[levels:]
    lat_index = lax.axis_index("lat")
    row_place = jnp.arange(rows_here + 2 * rim_width, dtype=jnp.int32)
    outside = (row_place < rim_width) & (lat_index == 0) | (row_place >= rows_here + rim_width) & (
        lat_index == lat_count - 1
    )
    inside = jnp.where(outside, 0.0, 1.0).astype(jnp.float32)[:, None]
    sea_rim = padded[0] * inside
    east_face = padded[1][:, :-1] * sea_rim[:, :-1] * sea_rim[:, 1:]
    north_face = padded[2][:-1, :] * sea_rim[:-1, :] * sea_rim[1:, :]
    for step_number in range(PASSES):
        field = one_pass(field, east_face, north_face, step_number)
    gradient = field
    return gradient


def solution(mesh):
    placed = (
        P(None, "lat", "lon"),
        P("lat", "lon"),
        P("lat", "lon"),
        P("lat", "lon"),
        P("lat", "lon"),
        P("lat", "lon"),
        P(None, "lat", "lon"),
        P(None, "lat", "lon"),
    )
    return jax.shard_map(
        body, mesh=mesh, in_specs=placed, out_specs=P(None, "lat", "lon"), check_vma=False
    )
```

```python
import jax
import jax.numpy as jnp
from jax import lax
from jax.experimental import pallas as pl
from jax.experimental.pallas import tpu as pltpu
from jax.sharding import PartitionSpec as P

PASSES = 8
CHUNK = 512
SCATTER_CHUNK = 1024


def three_parts(x):
    high = x.astype(jnp.bfloat16)
    rest = x - high.astype(jnp.float32)
    middle = rest.astype(jnp.bfloat16)
    low = (rest - middle.astype(jnp.float32)).astype(jnp.bfloat16)
    return high, middle, low


def scatter_kernel(held_ref, seen_ref, usable_ref, rows_ref, cols_ref, sea_ref, out_ref, acc_ref):
    levels, slots = seen_ref.shape
    peers, _, pair = held_ref.shape
    capacity = pair // 2
    per_chunk = SCATTER_CHUNK // capacity
    _, rows_here, cols_here = out_ref.shape
    cells = levels * rows_here
    acc_ref[...] = jnp.zeros_like(acc_ref)

    def step(k, carry):
        start = pl.multiple_of(k * SCATTER_CHUNK, SCATTER_CHUNK)
        here = pl.ds(start, SCATTER_CHUNK)
        held = [held_ref[k * per_chunk + i] for i in range(per_chunk)]
        values = jnp.concatenate([h[:, :capacity] for h in held], axis=1)
        weights = jnp.concatenate([h[:, capacity:] for h in held], axis=1)
        w = weights * (values - seen_ref[:, here]) * usable_ref[:, here]
        row_hit = lax.broadcasted_iota(jnp.int32, (rows_here, SCATTER_CHUNK), 0) == rows_ref[:, here]
        col_hit = lax.broadcasted_iota(jnp.int32, (cols_here, SCATTER_CHUNK), 0) == cols_ref[:, here]
        col_hit = col_hit.astype(jnp.float32).astype(jnp.bfloat16)
        spread = [
            jnp.where(row_hit[None], part.astype(jnp.float32)[:, None, :], 0.0)
            .reshape(cells, SCATTER_CHUNK)
            .astype(jnp.bfloat16)
            for part in three_parts(w)
        ]
        acc_ref[...] += lax.dot_general(
            jnp.concatenate(spread, axis=1),
            jnp.concatenate([col_hit] * 3, axis=1),
            (((1,), (1,)), ((), ())),
            preferred_element_type=jnp.float32,
        )
        return carry

    lax.fori_loop(0, slots // SCATTER_CHUNK, step, 0)
    out_ref[...] = acc_ref[...].reshape(levels, rows_here, cols_here) * sea_ref[...][None]


def gather_kernel(state_ref, rows_ref, cols_ref, out_ref):
    levels, slots = out_ref.shape
    cells, cols_here = state_ref.shape
    rows_here = cells // levels
    parts = three_parts(state_ref[...])

    def step(k, carry):
        start = pl.multiple_of(k * CHUNK, CHUNK)
        col_hit = lax.broadcasted_iota(jnp.int32, (cols_here, CHUNK), 0) == cols_ref[:, pl.ds(start, CHUNK)]
        col_hit = col_hit.astype(jnp.float32).astype(jnp.bfloat16)
        picked = None
        for part in parts:
            term = jnp.dot(part, col_hit, preferred_element_type=jnp.float32)
            picked = term if picked is None else picked + term
        row_hit = lax.broadcasted_iota(jnp.int32, (rows_here, CHUNK), 0) == rows_ref[:, pl.ds(start, CHUNK)]
        chosen = jnp.where(row_hit[None], picked.reshape(levels, rows_here, CHUNK), 0.0)
        out_ref[:, pl.ds(start, CHUNK)] = jnp.sum(chosen, axis=1)
        return carry

    lax.fori_loop(0, slots // CHUNK, step, 0)


def vmem_call(kernel, out_shape, flops, nbytes):
    return pl.pallas_call(
        kernel,
        out_shape=out_shape,
        in_specs=[pl.BlockSpec(memory_space=pltpu.VMEM)] * 3,
        out_specs=pl.BlockSpec(memory_space=pltpu.VMEM),
        cost_estimate=pl.CostEstimate(flops=flops, bytes_accessed=nbytes, transcendentals=0),
    )


def onehot_scatter(held, seen, usable, rows, cols, sea):
    levels, slots = seen.shape
    rows_here, cols_here = sea.shape
    shape = jax.ShapeDtypeStruct((levels, rows_here, cols_here), jnp.float32)
    flops = 6 * levels * rows_here * cols_here * slots
    return pl.pallas_call(
        scatter_kernel,
        out_shape=shape,
        in_specs=[pl.BlockSpec(memory_space=pltpu.VMEM)] * 6,
        out_specs=pl.BlockSpec(memory_space=pltpu.VMEM),
        scratch_shapes=[pltpu.VMEM((levels * rows_here, cols_here), jnp.float32)],
        cost_estimate=pl.CostEstimate(
            flops=flops, bytes_accessed=4 * (3 * levels * slots + 3 * slots + levels * rows_here * cols_here),
            transcendentals=0,
        ),
    )(held, seen, usable, rows, cols, sea)


def onehot_gather(state2d, rows, cols, levels):
    cells, cols_here = state2d.shape
    slots = rows.shape[1]
    shape = jax.ShapeDtypeStruct((levels, slots), jnp.float32)
    flops = 6 * cells * cols_here * slots
    return vmem_call(gather_kernel, shape, flops, 4 * (levels * slots + 2 * slots + cells * cols_here))(state2d, rows, cols)


def with_halo(block, sides, width):
    for axis, dim in sides:
        count = lax.axis_size(axis)
        forward = [(i, i + 1) for i in range(count - 1)]
        forward.append((count - 1, 0))
        backward = [(target, source) for source, target in forward]
        low = lax.slice_in_dim(block, block.shape[dim] - width, None, axis=dim)
        high = lax.slice_in_dim(block, 0, width, axis=dim)
        if dim == block.ndim - 1:
            flat = block.shape[:-2] + (-1,)
            low = lax.ppermute(low.reshape(flat), axis, forward).reshape(low.shape)
            high = lax.ppermute(high.reshape(flat), axis, backward).reshape(high.shape)
        else:
            low = lax.ppermute(low, axis, forward)
            high = lax.ppermute(high, axis, backward)
        block = jnp.concatenate([low, block, high], axis=dim)
    return block


def one_pass(field, east_face, north_face, offset):
    high, wide = field.shape[1], field.shape[2]
    rows = slice(offset + 1, offset + high - 1)
    cols = slice(offset + 1, offset + wide - 1)
    centre = field[:, 1:-1, 1:-1]
    east_here = east_face[rows, cols]
    east_west = east_face[rows, offset : offset + wide - 2]
    north_here = north_face[rows, cols]
    north_south = north_face[offset : offset + high - 2, cols]
    return (
        centre
        + east_here * (field[:, 1:-1, 2:] - centre)
        - east_west * (centre - field[:, 1:-1, :-2])
        + north_here * (field[:, 2:, 1:-1] - centre)
        - north_south * (centre - field[:, :-2, 1:-1])
    )


def body(state, coef_lon, coef_lat, land_sea, send_cols, send_count, obs_value, obs_weight):
    levels, rows_here, cols_here = state.shape
    lon_count = lax.axis_size("lon")
    lat_count = lax.axis_size("lat")
    slots = send_cols.shape[1]
    capacity = slots // lon_count
    targets = send_cols[0]
    slot_index = jnp.arange(slots, dtype=jnp.int32)
    limits = jnp.broadcast_to(send_count[0][:, None], (lon_count, capacity)).reshape(slots)
    usable = jnp.where(slot_index % capacity < limits, 1.0, 0.0).astype(jnp.float32)
    chunked = (levels, lon_count, capacity)
    held = jnp.concatenate([obs_value.reshape(chunked), obs_weight.reshape(chunked)], axis=2)
    held = jnp.transpose(held, (1, 0, 2))
    at_owner = lax.all_to_all(held, "lon", split_axis=0, concat_axis=0, tiled=True)
    target_rows = (targets // cols_here)[None, :]
    target_cols = (targets % cols_here)[None, :]
    at_column = onehot_gather(state.reshape(levels * rows_here, cols_here), target_rows, target_cols, levels)
    sea = land_sea.astype(jnp.float32)
    gradient = onehot_scatter(at_owner, at_column, usable[None, :], target_rows, target_cols, sea)
    rim_width = PASSES
    stacked = jnp.concatenate([gradient, sea[None], coef_lon[None], coef_lat[None]], axis=0)
    padded = with_halo(stacked, (("lat", 1), ("lon", 2)), rim_width)
    field = padded[:levels]
    padded = padded[levels:]
    lat_index = lax.axis_index("lat")
    row_place = jnp.arange(rows_here + 2 * rim_width, dtype=jnp.int32)
    outside = (row_place < rim_width) & (lat_index == 0) | (row_place >= rows_here + rim_width) & (
        lat_index == lat_count - 1
    )
    inside = jnp.where(outside, 0.0, 1.0).astype(jnp.float32)[:, None]
    sea_rim = padded[0] * inside
    east_face = padded[1][:, :-1] * sea_rim[:, :-1] * sea_rim[:, 1:]
    north_face = padded[2][:-1, :] * sea_rim[:-1, :] * sea_rim[1:, :]
    for step_number in range(PASSES):
        field = one_pass(field, east_face, north_face, step_number)
    gradient = field
    return gradient


def solution(mesh):
    placed = (
        P(None, "lat", "lon"),
        P("lat", "lon"),
        P("lat", "lon"),
        P("lat", "lon"),
        P("lat", "lon"),
        P("lat", "lon"),
        P(None, "lat", "lon"),
        P(None, "lat", "lon"),
    )
    return jax.shard_map(
        body, mesh=mesh, in_specs=placed, out_specs=P(None, "lat", "lon"), check_vma=False
    )
```

```python
import jax
import jax.numpy as jnp
from jax import lax
from jax.experimental import pallas as pl
from jax.experimental.pallas import tpu as pltpu
from jax.sharding import PartitionSpec as P

PASSES = 8
CHUNK = 512
SCATTER_CHUNK = 1024


def three_parts(x):
    high = x.astype(jnp.bfloat16)
    rest = x - high.astype(jnp.float32)
    middle = rest.astype(jnp.bfloat16)
    low = (rest - middle.astype(jnp.float32)).astype(jnp.bfloat16)
    return high, middle, low


def scatter_kernel(held_ref, seen_ref, usable_ref, rows_ref, cols_ref, sea_ref, out_ref, acc_ref):
    levels, slots = seen_ref.shape
    peers, _, pair = held_ref.shape
    capacity = pair // 2
    per_chunk = SCATTER_CHUNK // capacity
    _, rows_here, cols_here = out_ref.shape
    cells = levels * rows_here
    acc_ref[...] = jnp.zeros_like(acc_ref)

    def step(k, carry):
        start = pl.multiple_of(k * SCATTER_CHUNK, SCATTER_CHUNK)
        here = pl.ds(start, SCATTER_CHUNK)
        held = [held_ref[k * per_chunk + i] for i in range(per_chunk)]
        values = jnp.concatenate([h[:, :capacity] for h in held], axis=1)
        weights = jnp.concatenate([h[:, capacity:] for h in held], axis=1)
        w = weights * (values - seen_ref[:, here]) * usable_ref[:, here]
        row_hit = lax.broadcasted_iota(jnp.int32, (rows_here, SCATTER_CHUNK), 0) == rows_ref[:, here]
        col_hit = lax.broadcasted_iota(jnp.int32, (cols_here, SCATTER_CHUNK), 0) == cols_ref[:, here]
        col_hit = col_hit.astype(jnp.float32).astype(jnp.bfloat16)
        spread = [
            jnp.where(row_hit[None], part.astype(jnp.float32)[:, None, :], 0.0)
            .reshape(cells, SCATTER_CHUNK)
            .astype(jnp.bfloat16)
            for part in three_parts(w)
        ]
        acc_ref[...] += lax.dot_general(
            jnp.concatenate(spread, axis=1),
            jnp.concatenate([col_hit] * 3, axis=1),
            (((1,), (1,)), ((), ())),
            preferred_element_type=jnp.float32,
        )
        return carry

    lax.fori_loop(0, slots // SCATTER_CHUNK, step, 0)
    out_ref[...] = acc_ref[...].reshape(levels, rows_here, cols_here) * sea_ref[...][None]


def gather_kernel(state_ref, rows_ref, cols_ref, out_ref):
    levels, slots = out_ref.shape
    cells, cols_here = state_ref.shape
    rows_here = cells // levels
    parts = three_parts(state_ref[...])

    def step(k, carry):
        start = pl.multiple_of(k * CHUNK, CHUNK)
        col_hit = lax.broadcasted_iota(jnp.int32, (cols_here, CHUNK), 0) == cols_ref[:, pl.ds(start, CHUNK)]
        col_hit = col_hit.astype(jnp.float32).astype(jnp.bfloat16)
        picked = None
        for part in parts:
            term = jnp.dot(part, col_hit, preferred_element_type=jnp.float32)
            picked = term if picked is None else picked + term
        row_hit = lax.broadcasted_iota(jnp.int32, (rows_here, CHUNK), 0) == rows_ref[:, pl.ds(start, CHUNK)]
        chosen = jnp.where(row_hit[None], picked.reshape(levels, rows_here, CHUNK), 0.0)
        out_ref[:, pl.ds(start, CHUNK)] = jnp.sum(chosen, axis=1)
        return carry

    lax.fori_loop(0, slots // CHUNK, step, 0)


def vmem_call(kernel, out_shape, flops, nbytes):
    return pl.pallas_call(
        kernel,
        out_shape=out_shape,
        in_specs=[pl.BlockSpec(memory_space=pltpu.VMEM)] * 3,
        out_specs=pl.BlockSpec(memory_space=pltpu.VMEM),
        cost_estimate=pl.CostEstimate(flops=flops, bytes_accessed=nbytes, transcendentals=0),
    )


def onehot_scatter(held, seen, usable, rows, cols, sea):
    levels, slots = seen.shape
    rows_here, cols_here = sea.shape
    shape = jax.ShapeDtypeStruct((levels, rows_here, cols_here), jnp.float32)
    flops = 6 * levels * rows_here * cols_here * slots
    return pl.pallas_call(
        scatter_kernel,
        out_shape=shape,
        in_specs=[pl.BlockSpec(memory_space=pltpu.VMEM)] * 6,
        out_specs=pl.BlockSpec(memory_space=pltpu.VMEM),
        scratch_shapes=[pltpu.VMEM((levels * rows_here, cols_here), jnp.float32)],
        cost_estimate=pl.CostEstimate(
            flops=flops, bytes_accessed=4 * (3 * levels * slots + 3 * slots + levels * rows_here * cols_here),
            transcendentals=0,
        ),
    )(held, seen, usable, rows, cols, sea)


def onehot_gather(state2d, rows, cols, levels):
    cells, cols_here = state2d.shape
    slots = rows.shape[1]
    shape = jax.ShapeDtypeStruct((levels, slots), jnp.float32)
    flops = 6 * cells * cols_here * slots
    return vmem_call(gather_kernel, shape, flops, 4 * (levels * slots + 2 * slots + cells * cols_here))(state2d, rows, cols)


def with_halo(block, sides, width):
    for axis, dim in sides:
        count = lax.axis_size(axis)
        forward = [(i, i + 1) for i in range(count - 1)]
        forward.append((count - 1, 0))
        backward = [(target, source) for source, target in forward]
        low = lax.slice_in_dim(block, block.shape[dim] - width, None, axis=dim)
        high = lax.slice_in_dim(block, 0, width, axis=dim)
        if dim == block.ndim - 1:
            flat = (-1, 128) if low.size % 128 == 0 else block.shape[:-2] + (-1,)
            low = lax.ppermute(low.reshape(flat), axis, forward).reshape(low.shape)
            high = lax.ppermute(high.reshape(flat), axis, backward).reshape(high.shape)
        else:
            low = lax.ppermute(low, axis, forward)
            high = lax.ppermute(high, axis, backward)
        block = jnp.concatenate([low, block, high], axis=dim)
    return block


def one_pass(field, east_face, north_face, offset):
    high, wide = field.shape[1], field.shape[2]
    rows = slice(offset + 1, offset + high - 1)
    cols = slice(offset + 1, offset + wide - 1)
    centre = field[:, 1:-1, 1:-1]
    east_here = east_face[rows, cols]
    east_west = east_face[rows, offset : offset + wide - 2]
    north_here = north_face[rows, cols]
    north_south = north_face[offset : offset + high - 2, cols]
    return (
        centre
        + east_here * (field[:, 1:-1, 2:] - centre)
        - east_west * (centre - field[:, 1:-1, :-2])
        + north_here * (field[:, 2:, 1:-1] - centre)
        - north_south * (centre - field[:, :-2, 1:-1])
    )


def body(state, coef_lon, coef_lat, land_sea, send_cols, send_count, obs_value, obs_weight):
    levels, rows_here, cols_here = state.shape
    lon_count = lax.axis_size("lon")
    lat_count = lax.axis_size("lat")
    slots = send_cols.shape[1]
    capacity = slots // lon_count
    targets = send_cols[0]
    slot_index = jnp.arange(slots, dtype=jnp.int32)
    limits = jnp.broadcast_to(send_count[0][:, None], (lon_count, capacity)).reshape(slots)
    usable = jnp.where(slot_index % capacity < limits, 1.0, 0.0).astype(jnp.float32)
    chunked = (levels, lon_count, capacity)
    held = jnp.concatenate([obs_value.reshape(chunked), obs_weight.reshape(chunked)], axis=2)
    held = jnp.transpose(held, (1, 0, 2))
    at_owner = lax.all_to_all(held, "lon", split_axis=0, concat_axis=0, tiled=True)
    target_rows = (targets // cols_here)[None, :]
    target_cols = (targets % cols_here)[None, :]
    at_column = onehot_gather(state.reshape(levels * rows_here, cols_here), target_rows, target_cols, levels)
    sea = land_sea.astype(jnp.float32)
    gradient = onehot_scatter(at_owner, at_column, usable[None, :], target_rows, target_cols, sea)
    rim_width = PASSES
    stacked = jnp.concatenate([gradient, sea[None], coef_lon[None], coef_lat[None]], axis=0)
    padded = with_halo(stacked, (("lat", 1), ("lon", 2)), rim_width)
    field = padded[:levels]
    padded = padded[levels:]
    lat_index = lax.axis_index("lat")
    row_place = jnp.arange(rows_here + 2 * rim_width, dtype=jnp.int32)
    outside = (row_place < rim_width) & (lat_index == 0) | (row_place >= rows_here + rim_width) & (
        lat_index == lat_count - 1
    )
    inside = jnp.where(outside, 0.0, 1.0).astype(jnp.float32)[:, None]
    sea_rim = padded[0] * inside
    east_face = padded[1][:, :-1] * sea_rim[:, :-1] * sea_rim[:, 1:]
    north_face = padded[2][:-1, :] * sea_rim[:-1, :] * sea_rim[1:, :]
    for step_number in range(PASSES):
        field = one_pass(field, east_face, north_face, step_number)
    gradient = field
    return gradient


def solution(mesh):
    placed = (
        P(None, "lat", "lon"),
        P("lat", "lon"),
        P("lat", "lon"),
        P("lat", "lon"),
        P("lat", "lon"),
        P("lat", "lon"),
        P(None, "lat", "lon"),
        P(None, "lat", "lon"),
    )
    return jax.shard_map(
        body, mesh=mesh, in_specs=placed, out_specs=P(None, "lat", "lon"), check_vma=False
    )
```

```python
import jax
import jax.numpy as jnp
from jax import lax
from jax.experimental import pallas as pl
from jax.experimental.pallas import tpu as pltpu
from jax.sharding import PartitionSpec as P

PASSES = 8
CHUNK = 512
SCATTER_CHUNK = 1024


def three_parts(x):
    high = x.astype(jnp.bfloat16)
    rest = x - high.astype(jnp.float32)
    middle = rest.astype(jnp.bfloat16)
    low = (rest - middle.astype(jnp.float32)).astype(jnp.bfloat16)
    return high, middle, low


def scatter_kernel(held_ref, seen_ref, usable_ref, rows_ref, cols_ref, sea_ref, out_ref, acc_ref):
    levels, slots = seen_ref.shape
    peers, _, pair = held_ref.shape
    capacity = pair // 2
    per_chunk = SCATTER_CHUNK // capacity
    _, rows_here, cols_here = out_ref.shape
    cells = levels * rows_here
    acc_ref[...] = jnp.zeros_like(acc_ref)

    def step(k, carry):
        start = pl.multiple_of(k * SCATTER_CHUNK, SCATTER_CHUNK)
        here = pl.ds(start, SCATTER_CHUNK)
        held = [held_ref[k * per_chunk + i] for i in range(per_chunk)]
        values = jnp.concatenate([h[:, :capacity] for h in held], axis=1)
        weights = jnp.concatenate([h[:, capacity:] for h in held], axis=1)
        w = weights * (values - seen_ref[:, here]) * usable_ref[:, here]
        row_hit = lax.broadcasted_iota(jnp.int32, (rows_here, SCATTER_CHUNK), 0) == rows_ref[:, here]
        col_hit = lax.broadcasted_iota(jnp.int32, (cols_here, SCATTER_CHUNK), 0) == cols_ref[:, here]
        col_hit = col_hit.astype(jnp.float32).astype(jnp.bfloat16)
        spread = [
            jnp.where(row_hit[None], part.astype(jnp.float32)[:, None, :], 0.0)
            .reshape(cells, SCATTER_CHUNK)
            .astype(jnp.bfloat16)
            for part in three_parts(w)
        ]
        acc_ref[...] += lax.dot_general(
            jnp.concatenate(spread, axis=1),
            jnp.concatenate([col_hit] * 3, axis=1),
            (((1,), (1,)), ((), ())),
            preferred_element_type=jnp.float32,
        )
        return carry

    lax.fori_loop(0, slots // SCATTER_CHUNK, step, 0)
    out_ref[...] = acc_ref[...].reshape(levels, rows_here, cols_here) * sea_ref[...][None]


def gather_kernel(state_ref, rows_ref, cols_ref, out_ref):
    levels, slots = out_ref.shape
    cells, cols_here = state_ref.shape
    rows_here = cells // levels
    parts = three_parts(state_ref[...])

    def step(k, carry):
        start = pl.multiple_of(k * CHUNK, CHUNK)
        col_hit = lax.broadcasted_iota(jnp.int32, (cols_here, CHUNK), 0) == cols_ref[:, pl.ds(start, CHUNK)]
        col_hit = col_hit.astype(jnp.float32).astype(jnp.bfloat16)
        picked = None
        for part in parts:
            term = jnp.dot(part, col_hit, preferred_element_type=jnp.float32)
            picked = term if picked is None else picked + term
        row_hit = lax.broadcasted_iota(jnp.int32, (rows_here, CHUNK), 0) == rows_ref[:, pl.ds(start, CHUNK)]
        chosen = jnp.where(row_hit[None], picked.reshape(levels, rows_here, CHUNK), 0.0)
        out_ref[:, pl.ds(start, CHUNK)] = jnp.sum(chosen, axis=1)
        return carry

    lax.fori_loop(0, slots // CHUNK, step, 0)


def vmem_call(kernel, out_shape, flops, nbytes):
    return pl.pallas_call(
        kernel,
        out_shape=out_shape,
        in_specs=[pl.BlockSpec(memory_space=pltpu.VMEM)] * 3,
        out_specs=pl.BlockSpec(memory_space=pltpu.VMEM),
        cost_estimate=pl.CostEstimate(flops=flops, bytes_accessed=nbytes, transcendentals=0),
    )


def onehot_scatter(held, seen, usable, rows, cols, sea):
    levels, slots = seen.shape
    rows_here, cols_here = sea.shape
    shape = jax.ShapeDtypeStruct((levels, rows_here, cols_here), jnp.float32)
    flops = 6 * levels * rows_here * cols_here * slots
    return pl.pallas_call(
        scatter_kernel,
        out_shape=shape,
        in_specs=[pl.BlockSpec(memory_space=pltpu.VMEM)] * 6,
        out_specs=pl.BlockSpec(memory_space=pltpu.VMEM),
        scratch_shapes=[pltpu.VMEM((levels * rows_here, cols_here), jnp.float32)],
        cost_estimate=pl.CostEstimate(
            flops=flops, bytes_accessed=4 * (3 * levels * slots + 3 * slots + levels * rows_here * cols_here),
            transcendentals=0,
        ),
    )(held, seen, usable, rows, cols, sea)


def onehot_gather(state2d, rows, cols, levels):
    cells, cols_here = state2d.shape
    slots = rows.shape[1]
    shape = jax.ShapeDtypeStruct((levels, slots), jnp.float32)
    flops = 6 * cells * cols_here * slots
    return vmem_call(gather_kernel, shape, flops, 4 * (levels * slots + 2 * slots + cells * cols_here))(state2d, rows, cols)


def with_halo(planes, sides, width):
    block = None
    for axis, dim in sides:
        count = lax.axis_size(axis)
        forward = [(i, i + 1) for i in range(count - 1)]
        forward.append((count - 1, 0))
        backward = [(target, source) for source, target in forward]
        if block is None:
            low = jnp.concatenate([lax.slice_in_dim(p, p.shape[dim] - width, None, axis=dim) for p in planes])
            high = jnp.concatenate([lax.slice_in_dim(p, 0, width, axis=dim) for p in planes])
            block = jnp.concatenate(planes)
        else:
            low = lax.slice_in_dim(block, block.shape[dim] - width, None, axis=dim)
            high = lax.slice_in_dim(block, 0, width, axis=dim)
        if dim == block.ndim - 1:
            flat = (-1, 128) if low.size % 128 == 0 else block.shape[:-2] + (-1,)
            low = lax.ppermute(low.reshape(flat), axis, forward).reshape(low.shape)
            high = lax.ppermute(high.reshape(flat), axis, backward).reshape(high.shape)
        else:
            low = lax.ppermute(low, axis, forward)
            high = lax.ppermute(high, axis, backward)
        block = jnp.concatenate([low, block, high], axis=dim)
    return block


def one_pass(field, east_face, north_face, offset):
    high, wide = field.shape[1], field.shape[2]
    rows = slice(offset + 1, offset + high - 1)
    cols = slice(offset + 1, offset + wide - 1)
    centre = field[:, 1:-1, 1:-1]
    east_here = east_face[rows, cols]
    east_west = east_face[rows, offset : offset + wide - 2]
    north_here = north_face[rows, cols]
    north_south = north_face[offset : offset + high - 2, cols]
    return (
        centre
        + east_here * (field[:, 1:-1, 2:] - centre)
        - east_west * (centre - field[:, 1:-1, :-2])
        + north_here * (field[:, 2:, 1:-1] - centre)
        - north_south * (centre - field[:, :-2, 1:-1])
    )


def body(state, coef_lon, coef_lat, land_sea, send_cols, send_count, obs_value, obs_weight):
    levels, rows_here, cols_here = state.shape
    lon_count = lax.axis_size("lon")
    lat_count = lax.axis_size("lat")
    slots = send_cols.shape[1]
    capacity = slots // lon_count
    targets = send_cols[0]
    slot_index = jnp.arange(slots, dtype=jnp.int32)
    limits = jnp.broadcast_to(send_count[0][:, None], (lon_count, capacity)).reshape(slots)
    usable = jnp.where(slot_index % capacity < limits, 1.0, 0.0).astype(jnp.float32)
    chunked = (levels, lon_count, capacity)
    held = jnp.concatenate([obs_value.reshape(chunked), obs_weight.reshape(chunked)], axis=2)
    held = jnp.transpose(held, (1, 0, 2))
    at_owner = lax.all_to_all(held, "lon", split_axis=0, concat_axis=0, tiled=True)
    target_rows = (targets // cols_here)[None, :]
    target_cols = (targets % cols_here)[None, :]
    at_column = onehot_gather(state.reshape(levels * rows_here, cols_here), target_rows, target_cols, levels)
    sea = land_sea.astype(jnp.float32)
    gradient = onehot_scatter(at_owner, at_column, usable[None, :], target_rows, target_cols, sea)
    rim_width = PASSES
    padded = with_halo([gradient, sea[None], coef_lon[None], coef_lat[None]], (("lat", 1), ("lon", 2)), rim_width)
    field = padded[:levels]
    padded = padded[levels:]
    lat_index = lax.axis_index("lat")
    row_place = jnp.arange(rows_here + 2 * rim_width, dtype=jnp.int32)
    outside = (row_place < rim_width) & (lat_index == 0) | (row_place >= rows_here + rim_width) & (
        lat_index == lat_count - 1
    )
    inside = jnp.where(outside, 0.0, 1.0).astype(jnp.float32)[:, None]
    sea_rim = padded[0] * inside
    east_face = padded[1][:, :-1] * sea_rim[:, :-1] * sea_rim[:, 1:]
    north_face = padded[2][:-1, :] * sea_rim[:-1, :] * sea_rim[1:, :]
    for step_number in range(PASSES):
        field = one_pass(field, east_face, north_face, step_number)
    gradient = field
    return gradient


def solution(mesh):
    placed = (
        P(None, "lat", "lon"),
        P("lat", "lon"),
        P("lat", "lon"),
        P("lat", "lon"),
        P("lat", "lon"),
        P("lat", "lon"),
        P(None, "lat", "lon"),
        P(None, "lat", "lon"),
    )
    return jax.shard_map(
        body, mesh=mesh, in_specs=placed, out_specs=P(None, "lat", "lon"), check_vma=False
    )
```

```python
import functools

import jax
import jax.numpy as jnp
from jax import lax
from jax.experimental import pallas as pl
from jax.experimental.pallas import tpu as pltpu
from jax.sharding import PartitionSpec as P

PASSES = 8
CHUNK = 512
SCATTER_CHUNK = 1024


def three_parts(x):
    high = x.astype(jnp.bfloat16)
    rest = x - high.astype(jnp.float32)
    middle = rest.astype(jnp.bfloat16)
    low = (rest - middle.astype(jnp.float32)).astype(jnp.bfloat16)
    return high, middle, low


def scatter_kernel(row_starts, block_rows, held_ref, seen_ref, usable_ref, rows_ref, cols_ref, sea_ref, out_ref, acc_ref):
    levels, slots = seen_ref.shape
    peers, _, pair = held_ref.shape
    capacity = pair // 2
    per_chunk = SCATTER_CHUNK // capacity
    _, rows_here, cols_here = out_ref.shape
    cells = levels * rows_here
    acc_ref[...] = jnp.zeros_like(acc_ref)

    def step(k, carry):
        start = pl.multiple_of(k * SCATTER_CHUNK, SCATTER_CHUNK)
        here = pl.ds(start, SCATTER_CHUNK)
        held = [held_ref[k * per_chunk + i] for i in range(per_chunk)]
        values = jnp.concatenate([h[:, :capacity] for h in held], axis=1)
        weights = jnp.concatenate([h[:, capacity:] for h in held], axis=1)
        w = weights * (values - seen_ref[:, here]) * usable_ref[:, here]
        place = lax.broadcasted_iota(jnp.int32, (rows_here, SCATTER_CHUNK), 0)
        row_index = place + row_starts[0]
        for block, start_row in enumerate(row_starts[1:], 1):
            row_index = jnp.where(place >= block * block_rows, place - block * block_rows + start_row, row_index)
        row_hit = row_index == rows_ref[:, here]
        col_hit = lax.broadcasted_iota(jnp.int32, (cols_here, SCATTER_CHUNK), 0) == cols_ref[:, here]
        col_hit = col_hit.astype(jnp.float32).astype(jnp.bfloat16)
        spread = [
            jnp.where(row_hit[None], part.astype(jnp.float32)[:, None, :], 0.0)
            .reshape(cells, SCATTER_CHUNK)
            .astype(jnp.bfloat16)
            for part in three_parts(w)
        ]
        acc_ref[...] += lax.dot_general(
            jnp.concatenate(spread, axis=1),
            jnp.concatenate([col_hit] * 3, axis=1),
            (((1,), (1,)), ((), ())),
            preferred_element_type=jnp.float32,
        )
        return carry

    lax.fori_loop(0, slots // SCATTER_CHUNK, step, 0)
    out_ref[...] = acc_ref[...].reshape(levels, rows_here, cols_here) * sea_ref[...][None]


def gather_kernel(state_ref, rows_ref, cols_ref, out_ref):
    levels, slots = out_ref.shape
    cells, cols_here = state_ref.shape
    rows_here = cells // levels
    parts = three_parts(state_ref[...])

    def step(k, carry):
        start = pl.multiple_of(k * CHUNK, CHUNK)
        col_hit = lax.broadcasted_iota(jnp.int32, (cols_here, CHUNK), 0) == cols_ref[:, pl.ds(start, CHUNK)]
        col_hit = col_hit.astype(jnp.float32).astype(jnp.bfloat16)
        picked = None
        for part in parts:
            term = jnp.dot(part, col_hit, preferred_element_type=jnp.float32)
            picked = term if picked is None else picked + term
        row_hit = lax.broadcasted_iota(jnp.int32, (rows_here, CHUNK), 0) == rows_ref[:, pl.ds(start, CHUNK)]
        chosen = jnp.where(row_hit[None], picked.reshape(levels, rows_here, CHUNK), 0.0)
        out_ref[:, pl.ds(start, CHUNK)] = jnp.sum(chosen, axis=1)
        return carry

    lax.fori_loop(0, slots // CHUNK, step, 0)


def vmem_call(kernel, out_shape, flops, nbytes):
    return pl.pallas_call(
        kernel,
        out_shape=out_shape,
        in_specs=[pl.BlockSpec(memory_space=pltpu.VMEM)] * 3,
        out_specs=pl.BlockSpec(memory_space=pltpu.VMEM),
        cost_estimate=pl.CostEstimate(flops=flops, bytes_accessed=nbytes, transcendentals=0),
    )


def onehot_scatter(held, seen, usable, rows, cols, sea, row_starts, block_rows):
    levels, slots = seen.shape
    rows_here, cols_here = sea.shape
    shape = jax.ShapeDtypeStruct((levels, rows_here, cols_here), jnp.float32)
    flops = 6 * levels * rows_here * cols_here * slots
    return pl.pallas_call(
        functools.partial(scatter_kernel, row_starts, block_rows),
        out_shape=shape,
        in_specs=[pl.BlockSpec(memory_space=pltpu.VMEM)] * 6,
        out_specs=pl.BlockSpec(memory_space=pltpu.VMEM),
        scratch_shapes=[pltpu.VMEM((levels * rows_here, cols_here), jnp.float32)],
        cost_estimate=pl.CostEstimate(
            flops=flops, bytes_accessed=4 * (3 * levels * slots + 3 * slots + levels * rows_here * cols_here),
            transcendentals=0,
        ),
    )(held, seen, usable, rows, cols, sea)


def onehot_gather(state2d, rows, cols, levels):
    cells, cols_here = state2d.shape
    slots = rows.shape[1]
    shape = jax.ShapeDtypeStruct((levels, slots), jnp.float32)
    flops = 6 * cells * cols_here * slots
    return vmem_call(gather_kernel, shape, flops, 4 * (levels * slots + 2 * slots + cells * cols_here))(state2d, rows, cols)


def with_halo(planes, sides, width):
    block = None
    for axis, dim in sides:
        count = lax.axis_size(axis)
        forward = [(i, i + 1) for i in range(count - 1)]
        forward.append((count - 1, 0))
        backward = [(target, source) for source, target in forward]
        if block is None:
            low = jnp.concatenate([lax.slice_in_dim(p, p.shape[dim] - width, None, axis=dim) for p in planes])
            high = jnp.concatenate([lax.slice_in_dim(p, 0, width, axis=dim) for p in planes])
            block = jnp.concatenate(planes)
        else:
            low = lax.slice_in_dim(block, block.shape[dim] - width, None, axis=dim)
            high = lax.slice_in_dim(block, 0, width, axis=dim)
        if dim == block.ndim - 1:
            flat = (-1, 128) if low.size % 128 == 0 else block.shape[:-2] + (-1,)
            low = lax.ppermute(low.reshape(flat), axis, forward).reshape(low.shape)
            high = lax.ppermute(high.reshape(flat), axis, backward).reshape(high.shape)
        else:
            low = lax.ppermute(low, axis, forward)
            high = lax.ppermute(high, axis, backward)
        block = jnp.concatenate([low, block, high], axis=dim)
    return block


def one_pass(field, east_face, north_face, offset):
    high, wide = field.shape[1], field.shape[2]
    rows = slice(offset + 1, offset + high - 1)
    cols = slice(offset + 1, offset + wide - 1)
    centre = field[:, 1:-1, 1:-1]
    east_here = east_face[rows, cols]
    east_west = east_face[rows, offset : offset + wide - 2]
    north_here = north_face[rows, cols]
    north_south = north_face[offset : offset + high - 2, cols]
    return (
        centre
        + east_here * (field[:, 1:-1, 2:] - centre)
        - east_west * (centre - field[:, 1:-1, :-2])
        + north_here * (field[:, 2:, 1:-1] - centre)
        - north_south * (centre - field[:, :-2, 1:-1])
    )


def body(state, coef_lon, coef_lat, land_sea, send_cols, send_count, obs_value, obs_weight):
    levels, rows_here, cols_here = state.shape
    lon_count = lax.axis_size("lon")
    lat_count = lax.axis_size("lat")
    slots = send_cols.shape[1]
    capacity = slots // lon_count
    targets = send_cols[0]
    slot_index = jnp.arange(slots, dtype=jnp.int32)
    limits = jnp.broadcast_to(send_count[0][:, None], (lon_count, capacity)).reshape(slots)
    usable = jnp.where(slot_index % capacity < limits, 1.0, 0.0).astype(jnp.float32)
    chunked = (levels, lon_count, capacity)
    held = jnp.concatenate([obs_value.reshape(chunked), obs_weight.reshape(chunked)], axis=2)
    held = jnp.transpose(held, (1, 0, 2))
    at_owner = lax.all_to_all(held, "lon", split_axis=0, concat_axis=0, tiled=True)
    target_rows = (targets // cols_here)[None, :]
    target_cols = (targets % cols_here)[None, :]
    at_column = onehot_gather(state.reshape(levels * rows_here, cols_here), target_rows, target_cols, levels)
    sea = land_sea.astype(jnp.float32)
    rim_width = PASSES
    scatter_args = (at_owner, at_column, usable[None, :], target_rows, target_cols)
    edge_sea = jnp.concatenate([sea[:rim_width], sea[rows_here - rim_width :]])
    edge = onehot_scatter(*scatter_args, edge_sea, (0, rows_here - rim_width), rim_width)
    inner = onehot_scatter(
        *scatter_args, sea[rim_width : rows_here - rim_width], (rim_width,), rows_here - 2 * rim_width
    )
    lat_count_ = lax.axis_size("lat")
    up = [(i, (i + 1) % lat_count_) for i in range(lat_count_)]
    down = [(j, i) for i, j in up]
    extra = [sea[None], coef_lon[None], coef_lat[None]]
    low = jnp.concatenate([edge[:, rim_width:]] + [p[:, rows_here - rim_width :] for p in extra])
    high = jnp.concatenate([edge[:, :rim_width]] + [p[:, :rim_width] for p in extra])
    low = lax.ppermute(low, "lat", up)
    high = lax.ppermute(high, "lat", down)
    gradient = jnp.concatenate([edge[:, :rim_width], inner, edge[:, rim_width:]], axis=1)
    block = jnp.concatenate([gradient] + extra)
    block = jnp.concatenate([low, block, high], axis=1)
    padded = with_halo([block], (("lon", 2),), rim_width)
    field = padded[:levels]
    padded = padded[levels:]
    lat_index = lax.axis_index("lat")
    row_place = jnp.arange(rows_here + 2 * rim_width, dtype=jnp.int32)
    outside = (row_place < rim_width) & (lat_index == 0) | (row_place >= rows_here + rim_width) & (
        lat_index == lat_count - 1
    )
    inside = jnp.where(outside, 0.0, 1.0).astype(jnp.float32)[:, None]
    sea_rim = padded[0] * inside
    east_face = padded[1][:, :-1] * sea_rim[:, :-1] * sea_rim[:, 1:]
    north_face = padded[2][:-1, :] * sea_rim[:-1, :] * sea_rim[1:, :]
    for step_number in range(PASSES):
        field = one_pass(field, east_face, north_face, step_number)
    gradient = field
    return gradient


def solution(mesh):
    placed = (
        P(None, "lat", "lon"),
        P("lat", "lon"),
        P("lat", "lon"),
        P("lat", "lon"),
        P("lat", "lon"),
        P("lat", "lon"),
        P(None, "lat", "lon"),
        P(None, "lat", "lon"),
    )
    return jax.shard_map(
        body, mesh=mesh, in_specs=placed, out_specs=P(None, "lat", "lon"), check_vma=False
    )
```

```python
import jax
import jax.numpy as jnp
from jax import lax
from jax.experimental import pallas as pl
from jax.experimental.pallas import tpu as pltpu
from jax.sharding import PartitionSpec as P

PASSES = 8
CHUNK = 512
SCATTER_CHUNK = 2048


def three_parts(x):
    high = x.astype(jnp.bfloat16)
    rest = x - high.astype(jnp.float32)
    middle = rest.astype(jnp.bfloat16)
    low = (rest - middle.astype(jnp.float32)).astype(jnp.bfloat16)
    return high, middle, low


def scatter_kernel(held_ref, seen_ref, usable_ref, rows_ref, cols_ref, sea_ref, out_ref, acc_ref):
    levels, slots = seen_ref.shape
    peers, _, pair = held_ref.shape
    capacity = pair // 2
    per_chunk = SCATTER_CHUNK // capacity
    _, rows_here, cols_here = out_ref.shape
    cells = levels * rows_here
    acc_ref[...] = jnp.zeros_like(acc_ref)

    def step(k, carry):
        start = pl.multiple_of(k * SCATTER_CHUNK, SCATTER_CHUNK)
        here = pl.ds(start, SCATTER_CHUNK)
        held = [held_ref[k * per_chunk + i] for i in range(per_chunk)]
        values = jnp.concatenate([h[:, :capacity] for h in held], axis=1)
        weights = jnp.concatenate([h[:, capacity:] for h in held], axis=1)
        w = weights * (values - seen_ref[:, here]) * usable_ref[:, here]
        row_hit = lax.broadcasted_iota(jnp.int32, (rows_here, SCATTER_CHUNK), 0) == rows_ref[:, here]
        col_hit = lax.broadcasted_iota(jnp.int32, (cols_here, SCATTER_CHUNK), 0) == cols_ref[:, here]
        col_hit = col_hit.astype(jnp.float32).astype(jnp.bfloat16)
        spread = [
            jnp.where(row_hit[None], part.astype(jnp.float32)[:, None, :], 0.0)
            .reshape(cells, SCATTER_CHUNK)
            .astype(jnp.bfloat16)
            for part in three_parts(w)
        ]
        acc_ref[...] += lax.dot_general(
            jnp.concatenate(spread, axis=1),
            jnp.concatenate([col_hit] * 3, axis=1),
            (((1,), (1,)), ((), ())),
            preferred_element_type=jnp.float32,
        )
        return carry

    lax.fori_loop(0, slots // SCATTER_CHUNK, step, 0)
    out_ref[...] = acc_ref[...].reshape(levels, rows_here, cols_here) * sea_ref[...][None]


def gather_kernel(state_ref, rows_ref, cols_ref, out_ref):
    levels, slots = out_ref.shape
    cells, cols_here = state_ref.shape
    rows_here = cells // levels
    parts = three_parts(state_ref[...])

    def step(k, carry):
        start = pl.multiple_of(k * CHUNK, CHUNK)
        col_hit = lax.broadcasted_iota(jnp.int32, (cols_here, CHUNK), 0) == cols_ref[:, pl.ds(start, CHUNK)]
        col_hit = col_hit.astype(jnp.float32).astype(jnp.bfloat16)
        picked = None
        for part in parts:
            term = jnp.dot(part, col_hit, preferred_element_type=jnp.float32)
            picked = term if picked is None else picked + term
        row_hit = lax.broadcasted_iota(jnp.int32, (rows_here, CHUNK), 0) == rows_ref[:, pl.ds(start, CHUNK)]
        chosen = jnp.where(row_hit[None], picked.reshape(levels, rows_here, CHUNK), 0.0)
        out_ref[:, pl.ds(start, CHUNK)] = jnp.sum(chosen, axis=1)
        return carry

    lax.fori_loop(0, slots // CHUNK, step, 0)


def vmem_call(kernel, out_shape, flops, nbytes):
    return pl.pallas_call(
        kernel,
        out_shape=out_shape,
        in_specs=[pl.BlockSpec(memory_space=pltpu.VMEM)] * 3,
        out_specs=pl.BlockSpec(memory_space=pltpu.VMEM),
        cost_estimate=pl.CostEstimate(flops=flops, bytes_accessed=nbytes, transcendentals=0),
    )


def onehot_scatter(held, seen, usable, rows, cols, sea):
    levels, slots = seen.shape
    rows_here, cols_here = sea.shape
    shape = jax.ShapeDtypeStruct((levels, rows_here, cols_here), jnp.float32)
    flops = 6 * levels * rows_here * cols_here * slots
    return pl.pallas_call(
        scatter_kernel,
        out_shape=shape,
        in_specs=[pl.BlockSpec(memory_space=pltpu.VMEM)] * 6,
        out_specs=pl.BlockSpec(memory_space=pltpu.VMEM),
        scratch_shapes=[pltpu.VMEM((levels * rows_here, cols_here), jnp.float32)],
        cost_estimate=pl.CostEstimate(
            flops=flops, bytes_accessed=4 * (3 * levels * slots + 3 * slots + levels * rows_here * cols_here),
            transcendentals=0,
        ),
    )(held, seen, usable, rows, cols, sea)


def onehot_gather(state2d, rows, cols, levels):
    cells, cols_here = state2d.shape
    slots = rows.shape[1]
    shape = jax.ShapeDtypeStruct((levels, slots), jnp.float32)
    flops = 6 * cells * cols_here * slots
    return vmem_call(gather_kernel, shape, flops, 4 * (levels * slots + 2 * slots + cells * cols_here))(state2d, rows, cols)


def with_halo(block, sides, width):
    for axis, dim in sides:
        count = lax.axis_size(axis)
        forward = [(i, i + 1) for i in range(count - 1)]
        forward.append((count - 1, 0))
        backward = [(target, source) for source, target in forward]
        low = lax.slice_in_dim(block, block.shape[dim] - width, None, axis=dim)
        high = lax.slice_in_dim(block, 0, width, axis=dim)
        if dim == block.ndim - 1:
            flat = (-1, 128) if low.size % 128 == 0 else block.shape[:-2] + (-1,)
            low = lax.ppermute(low.reshape(flat), axis, forward).reshape(low.shape)
            high = lax.ppermute(high.reshape(flat), axis, backward).reshape(high.shape)
        else:
            low = lax.ppermute(low, axis, forward)
            high = lax.ppermute(high, axis, backward)
        block = jnp.concatenate([low, block, high], axis=dim)
    return block


def one_pass(field, east_face, north_face, offset):
    high, wide = field.shape[1], field.shape[2]
    rows = slice(offset + 1, offset + high - 1)
    cols = slice(offset + 1, offset + wide - 1)
    centre = field[:, 1:-1, 1:-1]
    east_here = east_face[rows, cols]
    east_west = east_face[rows, offset : offset + wide - 2]
    north_here = north_face[rows, cols]
    north_south = north_face[offset : offset + high - 2, cols]
    return (
        centre
        + east_here * (field[:, 1:-1, 2:] - centre)
        - east_west * (centre - field[:, 1:-1, :-2])
        + north_here * (field[:, 2:, 1:-1] - centre)
        - north_south * (centre - field[:, :-2, 1:-1])
    )


def body(state, coef_lon, coef_lat, land_sea, send_cols, send_count, obs_value, obs_weight):
    levels, rows_here, cols_here = state.shape
    lon_count = lax.axis_size("lon")
    lat_count = lax.axis_size("lat")
    slots = send_cols.shape[1]
    capacity = slots // lon_count
    targets = send_cols[0]
    slot_index = jnp.arange(slots, dtype=jnp.int32)
    limits = jnp.broadcast_to(send_count[0][:, None], (lon_count, capacity)).reshape(slots)
    usable = jnp.where(slot_index % capacity < limits, 1.0, 0.0).astype(jnp.float32)
    chunked = (levels, lon_count, capacity)
    held = jnp.concatenate([obs_value.reshape(chunked), obs_weight.reshape(chunked)], axis=2)
    held = jnp.transpose(held, (1, 0, 2))
    at_owner = lax.all_to_all(held, "lon", split_axis=0, concat_axis=0, tiled=True)
    target_rows = (targets // cols_here)[None, :]
    target_cols = (targets % cols_here)[None, :]
    at_column = onehot_gather(state.reshape(levels * rows_here, cols_here), target_rows, target_cols, levels)
    sea = land_sea.astype(jnp.float32)
    gradient = onehot_scatter(at_owner, at_column, usable[None, :], target_rows, target_cols, sea)
    rim_width = PASSES
    stacked = jnp.concatenate([gradient, sea[None], coef_lon[None], coef_lat[None]], axis=0)
    padded = with_halo(stacked, (("lat", 1), ("lon", 2)), rim_width)
    field = padded[:levels]
    padded = padded[levels:]
    lat_index = lax.axis_index("lat")
    row_place = jnp.arange(rows_here + 2 * rim_width, dtype=jnp.int32)
    outside = (row_place < rim_width) & (lat_index == 0) | (row_place >= rows_here + rim_width) & (
        lat_index == lat_count - 1
    )
    inside = jnp.where(outside, 0.0, 1.0).astype(jnp.float32)[:, None]
    sea_rim = padded[0] * inside
    east_face = padded[1][:, :-1] * sea_rim[:, :-1] * sea_rim[:, 1:]
    north_face = padded[2][:-1, :] * sea_rim[:-1, :] * sea_rim[1:, :]
    for step_number in range(PASSES):
        field = one_pass(field, east_face, north_face, step_number)
    gradient = field
    return gradient


def solution(mesh):
    placed = (
        P(None, "lat", "lon"),
        P("lat", "lon"),
        P("lat", "lon"),
        P("lat", "lon"),
        P("lat", "lon"),
        P("lat", "lon"),
        P(None, "lat", "lon"),
        P(None, "lat", "lon"),
    )
    return jax.shard_map(
        body, mesh=mesh, in_specs=placed, out_specs=P(None, "lat", "lon"), check_vma=False
    )
```

```python
import jax
import jax.numpy as jnp
from jax import lax
from jax.experimental import pallas as pl
from jax.experimental.pallas import tpu as pltpu
from jax.sharding import PartitionSpec as P

PASSES = 8
CHUNK = 512
SCATTER_CHUNK = 4096


def three_parts(x):
    high = x.astype(jnp.bfloat16)
    rest = x - high.astype(jnp.float32)
    middle = rest.astype(jnp.bfloat16)
    low = (rest - middle.astype(jnp.float32)).astype(jnp.bfloat16)
    return high, middle, low


def scatter_kernel(held_ref, seen_ref, usable_ref, rows_ref, cols_ref, sea_ref, out_ref, acc_ref):
    levels, slots = seen_ref.shape
    peers, _, pair = held_ref.shape
    capacity = pair // 2
    per_chunk = SCATTER_CHUNK // capacity
    _, rows_here, cols_here = out_ref.shape
    cells = levels * rows_here
    acc_ref[...] = jnp.zeros_like(acc_ref)

    def step(k, carry):
        start = pl.multiple_of(k * SCATTER_CHUNK, SCATTER_CHUNK)
        here = pl.ds(start, SCATTER_CHUNK)
        held = [held_ref[k * per_chunk + i] for i in range(per_chunk)]
        values = jnp.concatenate([h[:, :capacity] for h in held], axis=1)
        weights = jnp.concatenate([h[:, capacity:] for h in held], axis=1)
        w = weights * (values - seen_ref[:, here]) * usable_ref[:, here]
        row_hit = lax.broadcasted_iota(jnp.int32, (rows_here, SCATTER_CHUNK), 0) == rows_ref[:, here]
        col_hit = lax.broadcasted_iota(jnp.int32, (cols_here, SCATTER_CHUNK), 0) == cols_ref[:, here]
        col_hit = col_hit.astype(jnp.float32).astype(jnp.bfloat16)
        spread = [
            jnp.where(row_hit[None], part.astype(jnp.float32)[:, None, :], 0.0)
            .reshape(cells, SCATTER_CHUNK)
            .astype(jnp.bfloat16)
            for part in three_parts(w)
        ]
        acc_ref[...] += lax.dot_general(
            jnp.concatenate(spread, axis=1),
            jnp.concatenate([col_hit] * 3, axis=1),
            (((1,), (1,)), ((), ())),
            preferred_element_type=jnp.float32,
        )
        return carry

    lax.fori_loop(0, slots // SCATTER_CHUNK, step, 0)
    out_ref[...] = acc_ref[...].reshape(levels, rows_here, cols_here) * sea_ref[...][None]


def gather_kernel(state_ref, rows_ref, cols_ref, out_ref):
    levels, slots = out_ref.shape
    cells, cols_here = state_ref.shape
    rows_here = cells // levels
    parts = three_parts(state_ref[...])

    def step(k, carry):
        start = pl.multiple_of(k * CHUNK, CHUNK)
        col_hit = lax.broadcasted_iota(jnp.int32, (cols_here, CHUNK), 0) == cols_ref[:, pl.ds(start, CHUNK)]
        col_hit = col_hit.astype(jnp.float32).astype(jnp.bfloat16)
        picked = None
        for part in parts:
            term = jnp.dot(part, col_hit, preferred_element_type=jnp.float32)
            picked = term if picked is None else picked + term
        row_hit = lax.broadcasted_iota(jnp.int32, (rows_here, CHUNK), 0) == rows_ref[:, pl.ds(start, CHUNK)]
        chosen = jnp.where(row_hit[None], picked.reshape(levels, rows_here, CHUNK), 0.0)
        out_ref[:, pl.ds(start, CHUNK)] = jnp.sum(chosen, axis=1)
        return carry

    lax.fori_loop(0, slots // CHUNK, step, 0)


def vmem_call(kernel, out_shape, flops, nbytes):
    return pl.pallas_call(
        kernel,
        out_shape=out_shape,
        in_specs=[pl.BlockSpec(memory_space=pltpu.VMEM)] * 3,
        out_specs=pl.BlockSpec(memory_space=pltpu.VMEM),
        cost_estimate=pl.CostEstimate(flops=flops, bytes_accessed=nbytes, transcendentals=0),
    )


def onehot_scatter(held, seen, usable, rows, cols, sea):
    levels, slots = seen.shape
    rows_here, cols_here = sea.shape
    shape = jax.ShapeDtypeStruct((levels, rows_here, cols_here), jnp.float32)
    flops = 6 * levels * rows_here * cols_here * slots
    return pl.pallas_call(
        scatter_kernel,
        out_shape=shape,
        in_specs=[pl.BlockSpec(memory_space=pltpu.VMEM)] * 6,
        out_specs=pl.BlockSpec(memory_space=pltpu.VMEM),
        scratch_shapes=[pltpu.VMEM((levels * rows_here, cols_here), jnp.float32)],
        cost_estimate=pl.CostEstimate(
            flops=flops, bytes_accessed=4 * (3 * levels * slots + 3 * slots + levels * rows_here * cols_here),
            transcendentals=0,
        ),
    )(held, seen, usable, rows, cols, sea)


def onehot_gather(state2d, rows, cols, levels):
    cells, cols_here = state2d.shape
    slots = rows.shape[1]
    shape = jax.ShapeDtypeStruct((levels, slots), jnp.float32)
    flops = 6 * cells * cols_here * slots
    return vmem_call(gather_kernel, shape, flops, 4 * (levels * slots + 2 * slots + cells * cols_here))(state2d, rows, cols)


def with_halo(block, sides, width):
    for axis, dim in sides:
        count = lax.axis_size(axis)
        forward = [(i, i + 1) for i in range(count - 1)]
        forward.append((count - 1, 0))
        backward = [(target, source) for source, target in forward]
        low = lax.slice_in_dim(block, block.shape[dim] - width, None, axis=dim)
        high = lax.slice_in_dim(block, 0, width, axis=dim)
        if dim == block.ndim - 1:
            flat = (-1, 128) if low.size % 128 == 0 else block.shape[:-2] + (-1,)
            low = lax.ppermute(low.reshape(flat), axis, forward).reshape(low.shape)
            high = lax.ppermute(high.reshape(flat), axis, backward).reshape(high.shape)
        else:
            low = lax.ppermute(low, axis, forward)
            high = lax.ppermute(high, axis, backward)
        block = jnp.concatenate([low, block, high], axis=dim)
    return block


def one_pass(field, east_face, north_face, offset):
    high, wide = field.shape[1], field.shape[2]
    rows = slice(offset + 1, offset + high - 1)
    cols = slice(offset + 1, offset + wide - 1)
    centre = field[:, 1:-1, 1:-1]
    east_here = east_face[rows, cols]
    east_west = east_face[rows, offset : offset + wide - 2]
    north_here = north_face[rows, cols]
    north_south = north_face[offset : offset + high - 2, cols]
    return (
        centre
        + east_here * (field[:, 1:-1, 2:] - centre)
        - east_west * (centre - field[:, 1:-1, :-2])
        + north_here * (field[:, 2:, 1:-1] - centre)
        - north_south * (centre - field[:, :-2, 1:-1])
    )


def body(state, coef_lon, coef_lat, land_sea, send_cols, send_count, obs_value, obs_weight):
    levels, rows_here, cols_here = state.shape
    lon_count = lax.axis_size("lon")
    lat_count = lax.axis_size("lat")
    slots = send_cols.shape[1]
    capacity = slots // lon_count
    targets = send_cols[0]
    slot_index = jnp.arange(slots, dtype=jnp.int32)
    limits = jnp.broadcast_to(send_count[0][:, None], (lon_count, capacity)).reshape(slots)
    usable = jnp.where(slot_index % capacity < limits, 1.0, 0.0).astype(jnp.float32)
    chunked = (levels, lon_count, capacity)
    held = jnp.concatenate([obs_value.reshape(chunked), obs_weight.reshape(chunked)], axis=2)
    held = jnp.transpose(held, (1, 0, 2))
    at_owner = lax.all_to_all(held, "lon", split_axis=0, concat_axis=0, tiled=True)
    target_rows = (targets // cols_here)[None, :]
    target_cols = (targets % cols_here)[None, :]
    at_column = onehot_gather(state.reshape(levels * rows_here, cols_here), target_rows, target_cols, levels)
    sea = land_sea.astype(jnp.float32)
    gradient = onehot_scatter(at_owner, at_column, usable[None, :], target_rows, target_cols, sea)
    rim_width = PASSES
    stacked = jnp.concatenate([gradient, sea[None], coef_lon[None], coef_lat[None]], axis=0)
    padded = with_halo(stacked, (("lat", 1), ("lon", 2)), rim_width)
    field = padded[:levels]
    padded = padded[levels:]
    lat_index = lax.axis_index("lat")
    row_place = jnp.arange(rows_here + 2 * rim_width, dtype=jnp.int32)
    outside = (row_place < rim_width) & (lat_index == 0) | (row_place >= rows_here + rim_width) & (
        lat_index == lat_count - 1
    )
    inside = jnp.where(outside, 0.0, 1.0).astype(jnp.float32)[:, None]
    sea_rim = padded[0] * inside
    east_face = padded[1][:, :-1] * sea_rim[:, :-1] * sea_rim[:, 1:]
    north_face = padded[2][:-1, :] * sea_rim[:-1, :] * sea_rim[1:, :]
    for step_number in range(PASSES):
        field = one_pass(field, east_face, north_face, step_number)
    gradient = field
    return gradient


def solution(mesh):
    placed = (
        P(None, "lat", "lon"),
        P("lat", "lon"),
        P("lat", "lon"),
        P("lat", "lon"),
        P("lat", "lon"),
        P("lat", "lon"),
        P(None, "lat", "lon"),
        P(None, "lat", "lon"),
    )
    return jax.shard_map(
        body, mesh=mesh, in_specs=placed, out_specs=P(None, "lat", "lon"), check_vma=False
    )
```

```python
import jax
import jax.numpy as jnp
from jax import lax
from jax.experimental import pallas as pl
from jax.experimental.pallas import tpu as pltpu
from jax.sharding import PartitionSpec as P

PASSES = 8
CHUNK = 512
SCATTER_CHUNK = 2048


def three_parts(x):
    high = x.astype(jnp.bfloat16)
    rest = x - high.astype(jnp.float32)
    middle = rest.astype(jnp.bfloat16)
    low = (rest - middle.astype(jnp.float32)).astype(jnp.bfloat16)
    return high, middle, low


def scatter_kernel(held_ref, seen_ref, usable_ref, rows_ref, cols_ref, sea_ref, out_ref, acc_ref):
    levels, slots = seen_ref.shape
    peers, _, pair = held_ref.shape
    capacity = pair // 2
    per_chunk = SCATTER_CHUNK // capacity
    _, rows_here, cols_here = out_ref.shape
    cells = levels * rows_here
    acc_ref[...] = jnp.zeros_like(acc_ref)

    def step(k, carry):
        start = pl.multiple_of(k * SCATTER_CHUNK, SCATTER_CHUNK)
        here = pl.ds(start, SCATTER_CHUNK)
        held = [held_ref[k * per_chunk + i] for i in range(per_chunk)]
        values = jnp.concatenate([h[:, :capacity] for h in held], axis=1)
        weights = jnp.concatenate([h[:, capacity:] for h in held], axis=1)
        w = weights * (values - seen_ref[:, here]) * usable_ref[:, here]
        row_hit = lax.broadcasted_iota(jnp.int32, (rows_here, SCATTER_CHUNK), 0) == rows_ref[:, here]
        col_hit = lax.broadcasted_iota(jnp.int32, (cols_here, SCATTER_CHUNK), 0) == cols_ref[:, here]
        col_hit = col_hit.astype(jnp.float32).astype(jnp.bfloat16)
        spread = [
            jnp.where(row_hit[None], part.astype(jnp.float32)[:, None, :], 0.0)
            .reshape(cells, SCATTER_CHUNK)
            .astype(jnp.bfloat16)
            for part in three_parts(w)
        ]
        acc_ref[...] += lax.dot_general(
            jnp.concatenate(spread, axis=1),
            jnp.concatenate([col_hit] * 3, axis=1),
            (((1,), (1,)), ((), ())),
            preferred_element_type=jnp.float32,
        )
        return carry

    lax.fori_loop(0, slots // SCATTER_CHUNK, step, 0)
    out_ref[...] = acc_ref[...].reshape(levels, rows_here, cols_here) * sea_ref[...][None]


def gather_kernel(state_ref, rows_ref, cols_ref, out_ref):
    levels, slots = out_ref.shape
    cells, cols_here = state_ref.shape
    rows_here = cells // levels
    parts = three_parts(state_ref[...])

    def step(k, carry):
        start = pl.multiple_of(k * CHUNK, CHUNK)
        col_hit = lax.broadcasted_iota(jnp.int32, (cols_here, CHUNK), 0) == cols_ref[:, pl.ds(start, CHUNK)]
        col_hit = col_hit.astype(jnp.float32).astype(jnp.bfloat16)
        picked = None
        for part in parts:
            term = jnp.dot(part, col_hit, preferred_element_type=jnp.float32)
            picked = term if picked is None else picked + term
        row_hit = lax.broadcasted_iota(jnp.int32, (rows_here, CHUNK), 0) == rows_ref[:, pl.ds(start, CHUNK)]
        chosen = jnp.where(row_hit[None], picked.reshape(levels, rows_here, CHUNK), 0.0)
        out_ref[:, pl.ds(start, CHUNK)] = jnp.sum(chosen, axis=1)
        return carry

    lax.fori_loop(0, slots // CHUNK, step, 0)


def vmem_call(kernel, out_shape, flops, nbytes):
    return pl.pallas_call(
        kernel,
        out_shape=out_shape,
        in_specs=[pl.BlockSpec(memory_space=pltpu.VMEM)] * 3,
        out_specs=pl.BlockSpec(memory_space=pltpu.VMEM),
        cost_estimate=pl.CostEstimate(flops=flops, bytes_accessed=nbytes, transcendentals=0),
    )


def onehot_scatter(held, seen, usable, rows, cols, sea):
    levels, slots = seen.shape
    rows_here, cols_here = sea.shape
    shape = jax.ShapeDtypeStruct((levels, rows_here, cols_here), jnp.float32)
    flops = 6 * levels * rows_here * cols_here * slots
    return pl.pallas_call(
        scatter_kernel,
        out_shape=shape,
        in_specs=[pl.BlockSpec(memory_space=pltpu.VMEM)] * 6,
        out_specs=pl.BlockSpec(memory_space=pltpu.VMEM),
        scratch_shapes=[pltpu.VMEM((levels * rows_here, cols_here), jnp.float32)],
        cost_estimate=pl.CostEstimate(
            flops=flops, bytes_accessed=4 * (3 * levels * slots + 3 * slots + levels * rows_here * cols_here),
            transcendentals=0,
        ),
    )(held, seen, usable, rows, cols, sea)


def onehot_gather(state2d, rows, cols, levels):
    cells, cols_here = state2d.shape
    slots = rows.shape[1]
    shape = jax.ShapeDtypeStruct((levels, slots), jnp.float32)
    flops = 6 * cells * cols_here * slots
    return vmem_call(gather_kernel, shape, flops, 4 * (levels * slots + 2 * slots + cells * cols_here))(state2d, rows, cols)


def with_halo(block, sides, width):
    for axis, dim in sides:
        count = lax.axis_size(axis)
        forward = [(i, i + 1) for i in range(count - 1)]
        forward.append((count - 1, 0))
        backward = [(target, source) for source, target in forward]
        low = lax.slice_in_dim(block, block.shape[dim] - width, None, axis=dim)
        high = lax.slice_in_dim(block, 0, width, axis=dim)
        if dim == block.ndim - 1:
            flat = (-1, 128) if low.size % 128 == 0 else block.shape[:-2] + (-1,)
            low = lax.ppermute(low.reshape(flat), axis, forward).reshape(low.shape)
            high = lax.ppermute(high.reshape(flat), axis, backward).reshape(high.shape)
        else:
            low = lax.ppermute(low, axis, forward)
            high = lax.ppermute(high, axis, backward)
        block = jnp.concatenate([low, block, high], axis=dim)
    return block


def one_pass(field, faces, offset):
    high, wide = field.shape[1], field.shape[2]
    window = faces[:, offset + 1 : offset + high - 1, offset + 1 : offset + wide - 1]
    centre = field[:, 1:-1, 1:-1]
    return (
        centre
        + window[0] * (field[:, 1:-1, 2:] - centre)
        - window[1] * (centre - field[:, 1:-1, :-2])
        + window[2] * (field[:, 2:, 1:-1] - centre)
        - window[3] * (centre - field[:, :-2, 1:-1])
    )


def body(state, coef_lon, coef_lat, land_sea, send_cols, send_count, obs_value, obs_weight):
    levels, rows_here, cols_here = state.shape
    lon_count = lax.axis_size("lon")
    lat_count = lax.axis_size("lat")
    slots = send_cols.shape[1]
    capacity = slots // lon_count
    targets = send_cols[0]
    slot_index = jnp.arange(slots, dtype=jnp.int32)
    limits = jnp.broadcast_to(send_count[0][:, None], (lon_count, capacity)).reshape(slots)
    usable = jnp.where(slot_index % capacity < limits, 1.0, 0.0).astype(jnp.float32)
    chunked = (levels, lon_count, capacity)
    held = jnp.concatenate([obs_value.reshape(chunked), obs_weight.reshape(chunked)], axis=2)
    held = jnp.transpose(held, (1, 0, 2))
    at_owner = lax.all_to_all(held, "lon", split_axis=0, concat_axis=0, tiled=True)
    target_rows = (targets // cols_here)[None, :]
    target_cols = (targets % cols_here)[None, :]
    at_column = onehot_gather(state.reshape(levels * rows_here, cols_here), target_rows, target_cols, levels)
    sea = land_sea.astype(jnp.float32)
    gradient = onehot_scatter(at_owner, at_column, usable[None, :], target_rows, target_cols, sea)
    rim_width = PASSES
    stacked = jnp.concatenate([gradient, sea[None], coef_lon[None], coef_lat[None]], axis=0)
    padded = with_halo(stacked, (("lat", 1), ("lon", 2)), rim_width)
    field = padded[:levels]
    padded = padded[levels:]
    lat_index = lax.axis_index("lat")
    row_place = jnp.arange(rows_here + 2 * rim_width, dtype=jnp.int32)
    outside = (row_place < rim_width) & (lat_index == 0) | (row_place >= rows_here + rim_width) & (
        lat_index == lat_count - 1
    )
    inside = jnp.where(outside, 0.0, 1.0).astype(jnp.float32)[:, None]
    sea_rim = padded[0] * inside
    east_face = padded[1][:, :-1] * sea_rim[:, :-1] * sea_rim[:, 1:]
    north_face = padded[2][:-1, :] * sea_rim[:-1, :] * sea_rim[1:, :]
    high, wide = padded.shape[1], padded.shape[2]
    faces = jnp.stack(
        [
            jnp.pad(east_face, ((0, 0), (0, 1))),
            jnp.pad(east_face, ((0, 0), (1, 0))),
            jnp.pad(north_face, ((0, 1), (0, 0))),
            jnp.pad(north_face, ((1, 0), (0, 0))),
        ]
    )
    for step_number in range(PASSES):
        field = one_pass(field, faces, step_number)
    gradient = field
    return gradient


def solution(mesh):
    placed = (
        P(None, "lat", "lon"),
        P("lat", "lon"),
        P("lat", "lon"),
        P("lat", "lon"),
        P("lat", "lon"),
        P("lat", "lon"),
        P(None, "lat", "lon"),
        P(None, "lat", "lon"),
    )
    return jax.shard_map(
        body, mesh=mesh, in_specs=placed, out_specs=P(None, "lat", "lon"), check_vma=False
    )
```
